512 devices in a mesh: col: 32 (over x_lo, z, core), rec: 16 (over x_hi, y).
Axes of the slice: x: 4 (x_hi: 2, x_lo: 2; x = x_hi * 2 + x_lo), y: 8, z: 8, core: 2. Of those that a mesh axis runs over, the one named last changes fastest.
Arguments:
- design: bfloat16 [4096, 16384], P('rec', 'col')
- record_weight: float32 [4096], P('rec'), may hold values from 0.5 to 3.47
Outputs:
- rotated_design: bfloat16 [4096, 16384], P('rec', 'col')
- column_rms: float32 [16384], P('col')
The draws below stay inside these ranges and needn't reach their ends.
All inputs are finite; a program needn't handle non-finite values.
Results may differ from the reference program's by a relative error of at most 0.0088.
Values may be sent and summed in bfloat16 or wider, within the bound.
No kernel may reach another device: no remote copies, remote signals or barrier semaphores. Data moves between devices by JAX's collectives and lax.ppermute only.
A program may use at most 64 MiB of HBM per device.

```python
import jax
import jax.numpy as jnp
from jax import lax

BW = 256
ROUNDS = 3
SWEEPS = 6
RECORDS = 4096
COLS = 16384


def draw_design(key, part):
    subkeys = jax.random.split(key, 5)
    noise_part = jax.random.normal(subkeys[0], (RECORDS, COLS), jnp.float32)
    common = 0.6
    banded = jnp.repeat(jax.random.normal(subkeys[1], (RECORDS, COLS // 16), jnp.float32), 16, axis=1)
    shared = jax.random.normal(subkeys[2], (RECORDS, 1), jnp.float32) * jax.random.normal(subkeys[3], (1, COLS), jnp.float32)
    scales = jnp.exp(jax.random.uniform(subkeys[4], (1, COLS), jnp.float32, 0.0, 2.3))
    return ((noise_part + 0.8 * banded + common * shared) * scales * 0.25).astype(jnp.bfloat16)


def draw_record_weight(key, part):
    ramp = jnp.sqrt(1.0 + 2.0 * jnp.arange(RECORDS, dtype=jnp.float32) / (RECORDS - 1))
    base_weight = jnp.exp(jax.random.uniform(key, (RECORDS,), jnp.float32, -0.6931, 0.6931))
    return base_weight * ramp


def setup_inputs(seed: int = 0) -> dict:
    keys = jax.random.split(jax.random.key(seed), 3)
    return {
        "design": draw_design(jax.random.fold_in(keys[2], 71), 0),
        "record_weight": draw_record_weight(jax.random.fold_in(keys[2], 71), 0),
    }


eps_angle = 0.01

def jacobi_sweeps(gram_matrix, width):
    top_left = gram_matrix[:width, :width]
    top_right = gram_matrix[:width, width:]
    low_left = gram_matrix[width:, :width]
    low_right = gram_matrix[width:, width:]
    identity = jnp.eye(2 * width, dtype=jnp.float32)
    rot_first = identity[:, :width]
    rot_second = identity[:, width:]
    for sweep_index in range(SWEEPS):
        if sweep_index > 0:
            top_right = jnp.roll(top_right, -1, axis=1)
            low_left = jnp.roll(low_left, -1, axis=0)
            low_right = jnp.roll(jnp.roll(low_right, -1, axis=0), -1, axis=1)
            rot_second = jnp.roll(rot_second, -1, axis=1)
        first_diag = jnp.diagonal(top_left)
        second_diag = jnp.diagonal(low_right)
        coupling = jnp.diagonal(top_right)
        spread = second_diag - first_diag
        tangent = 2.0 * coupling * spread / (spread * spread + 4.0 * coupling * coupling + eps_angle * (first_diag + second_diag) ** 2)
        half_angle = 0.5 * jnp.arctan(tangent)
        cosine = jnp.cos(half_angle)
        sine_value = jnp.sin(half_angle)
        cos_col = cosine[None, :]
        sin_col = sine_value[None, :]
        cos_row = cosine[:, None]
        sin_row = sine_value[:, None]
        left_a = top_left * cos_col - top_right * sin_col
        right_a = top_left * sin_col + top_right * cos_col
        left_b = low_left * cos_col - low_right * sin_col
        right_b = low_left * sin_col + low_right * cos_col
        top_left = cos_row * left_a - sin_row * left_b
        low_left = sin_row * left_a + cos_row * left_b
        top_right = cos_row * right_a - sin_row * right_b
        low_right = sin_row * right_a + cos_row * right_b
        rot_first, rot_second = (rot_first * cos_col - rot_second * sin_col, rot_first * sin_col + rot_second * cos_col)
    rot_second = jnp.roll(rot_second, SWEEPS - 1, axis=1)
    return jnp.concatenate([rot_first, rot_second], axis=1)

def one_pair(blocks):
    pair_data = jnp.concatenate([blocks[0], blocks[1]], axis=1)
    gram_matrix = jnp.dot(pair_data.T, pair_data, preferred_element_type=jnp.float32)
    rotation = jacobi_sweeps(gram_matrix, BW).astype(jnp.bfloat16)
    rotated = jnp.dot(pair_data, rotation, preferred_element_type=jnp.float32).astype(jnp.bfloat16)
    return (rotated[:, :BW], rotated[:, BW:])

def reference(design, record_weight):
    weighted = (design.astype(jnp.float32) * record_weight[:, None]).astype(jnp.bfloat16)
    pairs_count = COLS // (2 * BW)
    stacked = weighted.reshape(RECORDS, pairs_count, 2, BW)
    upper_blocks = jnp.transpose(stacked[:, :, 0, :], (1, 0, 2))
    lower_blocks = jnp.transpose(stacked[:, :, 1, :], (1, 0, 2))
    for round_index in range(ROUNDS):
        upper_blocks, lower_blocks = lax.map(one_pair, (upper_blocks, lower_blocks))
        if round_index + 1 < ROUNDS:
            moved_upper = jnp.concatenate([upper_blocks[:1], lower_blocks[:1], upper_blocks[1:-1]], axis=0)
            lower_blocks = jnp.concatenate([lower_blocks[1:], upper_blocks[-1:]], axis=0)
            upper_blocks = moved_upper
    final_blocks = jnp.stack([upper_blocks, lower_blocks], axis=1)
    rotated_design = jnp.transpose(final_blocks, (2, 0, 1, 3)).reshape(RECORDS, COLS)
    squares = lax.optimization_barrier(jnp.sum(jnp.square(rotated_design.astype(jnp.float32)), axis=0))
    column_rms = jnp.sqrt(squares / RECORDS + 1e-06)
    return (rotated_design, column_rms)
```

```python
import jax
import jax.numpy as jnp
from jax import lax
from jax.sharding import PartitionSpec as P

ROUNDS = 3
SWEEPS = 6


eps_angle = 0.01


def from_behind(value, axis, steps):
    count = lax.axis_size(axis)
    leading, last = (max(0, -steps), min(count, count - steps))
    return lax.ppermute(value, axis, [(source, source + steps) for source in range(leading, last)])


def diagonal_of(matrix):
    size = matrix.shape[0]
    rows = lax.broadcasted_iota(jnp.int32, (size, size), 0)
    cols = lax.broadcasted_iota(jnp.int32, (size, size), 1)
    return jnp.sum(jnp.where(rows == cols, matrix, 0.0), axis=0)


def jacobi_sweeps(gram_matrix, width):
    top_left = gram_matrix[:width, :width]
    top_right = gram_matrix[:width, width:]
    low_left = gram_matrix[width:, :width]
    low_right = gram_matrix[width:, width:]
    identity = jnp.eye(2 * width, dtype=jnp.float32)
    rot_first = identity[:, :width]
    rot_second = identity[:, width:]
    for sweep_index in range(SWEEPS):
        if sweep_index > 0:
            top_right = jnp.roll(top_right, -1, axis=1)
            low_left = jnp.roll(low_left, -1, axis=0)
            low_right = jnp.roll(jnp.roll(low_right, -1, axis=0), -1, axis=1)
            rot_second = jnp.roll(rot_second, -1, axis=1)
        first_diag = diagonal_of(top_left)
        second_diag = diagonal_of(low_right)
        coupling = diagonal_of(top_right)
        spread = second_diag - first_diag
        tangent = (
            2.0
            * coupling
            * spread
            / (
                spread * spread
                + 4.0 * coupling * coupling
                + eps_angle * (first_diag + second_diag) ** 2
            )
        )
        half_angle = 0.5 * jnp.arctan(tangent)
        cosine = jnp.cos(half_angle)
        sine_value = jnp.sin(half_angle)
        cos_col = cosine[None, :]
        sin_col = sine_value[None, :]
        cos_row = cosine[:, None]
        sin_row = sine_value[:, None]
        left_a = top_left * cos_col - top_right * sin_col
        right_a = top_left * sin_col + top_right * cos_col
        left_b = low_left * cos_col - low_right * sin_col
        right_b = low_left * sin_col + low_right * cos_col
        top_left = cos_row * left_a - sin_row * left_b
        low_left = sin_row * left_a + cos_row * left_b
        top_right = cos_row * right_a - sin_row * right_b
        low_right = sin_row * right_a + cos_row * right_b
        rot_first, rot_second = (
            rot_first * cos_col - rot_second * sin_col,
            rot_first * sin_col + rot_second * cos_col,
        )
    rot_second = jnp.roll(rot_second, SWEEPS - 1, axis=1)
    return jnp.concatenate([rot_first, rot_second], axis=1)


def send_right(block):
    return from_behind(block, "col", 1)


def send_left(block):
    return from_behind(block, "col", -1)


def inner_products(left_part, right_part):
    return lax.dot_general(
        left_part, right_part, (((0,), (0,)), ((), ())), preferred_element_type=jnp.float32
    )


def reduce_over_records(rows_in):
    count = lax.axis_size("rec")
    total, width = rows_in.shape
    chunks = rows_in.reshape(count, total // count, width)
    mine = lax.all_to_all(chunks, "rec", 0, 0, tiled=False).sum(axis=0)
    spread = jnp.broadcast_to(mine[None], (count,) + mine.shape)
    return lax.all_to_all(spread, "rec", 0, 0, tiled=False).reshape(total, width)


def summed_gram(pair_data, width):
    gram_local = inner_products(pair_data, pair_data)
    top_left = gram_local[:width, :width]
    top_right = gram_local[:width, width:]
    low_right = gram_local[width:, width:]
    rows = lax.broadcasted_iota(jnp.int32, (width, width), 0)
    cols = lax.broadcasted_iota(jnp.int32, (width, width), 1)
    folded = jnp.where(rows <= cols, top_left, low_right)
    count = lax.axis_size("rec")
    padded = -(-(2 * width + 1) // (8 * count)) * 8 * count
    packed = jnp.concatenate(
        [
            folded,
            top_right,
            diagonal_of(low_right)[None, :],
            jnp.zeros((padded - 2 * width - 1, width), jnp.float32),
        ],
        axis=0,
    )
    summed = reduce_over_records(packed)
    folded = summed[:width]
    top_right = summed[width : 2 * width]
    low_diag = summed[2 * width]
    mirrored = folded.T
    top_left = jnp.where(rows <= cols, folded, mirrored)
    low_right = jnp.where(rows > cols, folded, jnp.where(rows < cols, mirrored, low_diag[None, :]))
    return jnp.concatenate(
        [
            jnp.concatenate([top_left, top_right], axis=1),
            jnp.concatenate([top_right.T, low_right], axis=1),
        ],
        axis=0,
    )


def local(design, record_weight):
    width = design.shape[1] // 2
    weighted = (design.astype(jnp.float32) * record_weight[:, None]).astype(jnp.bfloat16)
    upper_block = weighted[:, :width]
    lower_block = weighted[:, width:]
    position = lax.axis_index("col")
    device_count = lax.axis_size("col")
    for round_index in range(ROUNDS):
        moving = round_index + 1 < ROUNDS
        pair_data = jnp.concatenate([upper_block, lower_block], axis=1)
        gram_matrix = summed_gram(pair_data, width)
        rotation = jacobi_sweeps(gram_matrix, width).astype(jnp.bfloat16)
        rotated = jnp.dot(pair_data, rotation, preferred_element_type=jnp.float32).astype(
            jnp.bfloat16
        )
        new_upper = rotated[:, :width]
        new_lower = rotated[:, width:]
        if moving:
            from_right = send_left(new_lower)
            from_left = send_right(jnp.where(position == 0, new_lower, new_upper))
        if moving:
            upper_block = jnp.where(position == 0, new_upper, from_left)
            lower_block = jnp.where(position == device_count - 1, new_upper, from_right)
        else:
            upper_block = new_upper
            lower_block = new_lower
    rotated_design = jnp.concatenate([upper_block, lower_block], axis=1)
    squares = jnp.sum(jnp.square(rotated_design.astype(jnp.float32)), axis=0)
    count = lax.axis_size("rec")
    spread = jnp.broadcast_to(squares[None], (count,) + squares.shape)
    totals = lax.all_to_all(spread, "rec", 0, 0, tiled=False).sum(axis=0)
    record_total = design.shape[0] * lax.axis_size("rec")
    column_rms = jnp.sqrt(totals / record_total + 1e-06)
    return (rotated_design, column_rms)


def solution(mesh):
    placed = (P("rec", "col"), P("rec"))
    return jax.shard_map(
        local, mesh=mesh, in_specs=placed, out_specs=(P("rec", "col"), P("col")), check_vma=False
    )
```

```python
import jax
import jax.numpy as jnp
from jax import lax
from jax.experimental import pallas as pl
from jax.experimental.pallas import tpu as pltpu
from jax.sharding import PartitionSpec as P

ROUNDS = 3
SWEEPS = 6


eps_angle = 0.01


def from_behind(value, axis, steps):
    count = lax.axis_size(axis)
    leading, last = (max(0, -steps), min(count, count - steps))
    return lax.ppermute(value, axis, [(source, source + steps) for source in range(leading, last)])


def diagonal_of(matrix):
    size = matrix.shape[0]
    rows = lax.broadcasted_iota(jnp.int32, (size, size), 0)
    cols = lax.broadcasted_iota(jnp.int32, (size, size), 1)
    return jnp.sum(jnp.where(rows == cols, matrix, 0.0), axis=0)


def half_angle_terms(first_diag, second_diag, coupling):
    spread = second_diag - first_diag
    tangent = (
        2.0
        * coupling
        * spread
        / (
            spread * spread
            + 4.0 * coupling * coupling
            + eps_angle * (first_diag + second_diag) ** 2
        )
    )
    double_cos = 1.0 / jnp.sqrt(1.0 + tangent * tangent)
    cosine = jnp.sqrt(0.5 + 0.5 * double_cos)
    sine_value = tangent * double_cos / (2.0 * cosine)
    return cosine, sine_value


def sweeps_kernel(top_left_ref, top_right_ref, low_left_ref, low_right_ref, rotation_ref):
    width = top_left_ref.shape[0]
    top_left = top_left_ref[...]
    top_right = top_right_ref[...]
    low_left = low_left_ref[...]
    low_right = low_right_ref[...]
    rows = lax.broadcasted_iota(jnp.int32, (width, width), 0)
    cols = lax.broadcasted_iota(jnp.int32, (width, width), 1)
    on_diagonal = rows == cols
    first_top = jnp.where(on_diagonal, 1.0, 0.0).astype(jnp.float32)
    first_low = jnp.zeros((width, width), jnp.float32)
    second_top = jnp.zeros((width, width), jnp.float32)
    second_low = first_top

    def both_diagonals(matrix):
        masked = jnp.where(on_diagonal, matrix, 0.0)
        return jnp.sum(masked, axis=0, keepdims=True), jnp.sum(masked, axis=1, keepdims=True)

    def to_left(matrix, axis):
        return pltpu.roll(matrix, width - 1, axis)

    for sweep_index in range(SWEEPS):
        if sweep_index > 0:
            top_right = to_left(top_right, 1)
            low_left = to_left(low_left, 0)
            low_right = to_left(to_left(low_right, 0), 1)
            second_top = to_left(second_top, 1)
            second_low = to_left(second_low, 1)
        first_r, first_c = both_diagonals(top_left)
        second_r, second_c = both_diagonals(low_right)
        coupling_r, coupling_c = both_diagonals(top_right)
        cos_col, sin_col = half_angle_terms(first_r, second_r, coupling_r)
        cos_row, sin_row = half_angle_terms(first_c, second_c, coupling_c)
        left_a = top_left * cos_col - top_right * sin_col
        right_a = top_left * sin_col + top_right * cos_col
        left_b = low_left * cos_col - low_right * sin_col
        right_b = low_left * sin_col + low_right * cos_col
        top_left = cos_row * left_a - sin_row * left_b
        low_left = sin_row * left_a + cos_row * left_b
        top_right = cos_row * right_a - sin_row * right_b
        low_right = sin_row * right_a + cos_row * right_b
        first_top, second_top = (
            first_top * cos_col - second_top * sin_col,
            first_top * sin_col + second_top * cos_col,
        )
        first_low, second_low = (
            first_low * cos_col - second_low * sin_col,
            first_low * sin_col + second_low * cos_col,
        )
    second_top = pltpu.roll(second_top, SWEEPS - 1, 1)
    second_low = pltpu.roll(second_low, SWEEPS - 1, 1)
    out = rotation_ref.dtype
    rotation_ref[:width, :width] = first_top.astype(out)
    rotation_ref[width:, :width] = first_low.astype(out)
    rotation_ref[:width, width:] = second_top.astype(out)
    rotation_ref[width:, width:] = second_low.astype(out)


def rotation_of(top_left, top_right, low_left, low_right):
    width = top_left.shape[0]
    vmem = pl.BlockSpec(memory_space=pltpu.VMEM)
    return pl.pallas_call(
        sweeps_kernel,
        out_shape=jax.ShapeDtypeStruct((2 * width, 2 * width), jnp.bfloat16),
        in_specs=[vmem] * 4,
        out_specs=vmem,
        cost_estimate=pl.CostEstimate(
            flops=SWEEPS * 40 * width * width, transcendentals=SWEEPS * 8 * width, bytes_accessed=5 * 4 * width * width
        ),
    )(top_left, top_right, low_left, low_right)


def send_right(block):
    return from_behind(block, "col", 1)


def send_left(block):
    return from_behind(block, "col", -1)


def inner_products(left_part, right_part):
    return lax.dot_general(
        left_part, right_part, (((0,), (0,)), ((), ())), preferred_element_type=jnp.float32
    )


def reduce_over_records(rows_in):
    count = lax.axis_size("rec")
    total, width = rows_in.shape
    chunks = rows_in.reshape(count, total // count, width)
    mine = lax.all_to_all(chunks, "rec", 0, 0, tiled=False).sum(axis=0)
    spread = jnp.broadcast_to(mine[None], (count,) + mine.shape)
    return lax.all_to_all(spread, "rec", 0, 0, tiled=False).reshape(total, width)


def summed_gram(pair_data, width):
    gram_local = inner_products(pair_data, pair_data)
    top_left = gram_local[:width, :width]
    top_right = gram_local[:width, width:]
    low_right = gram_local[width:, width:]
    rows = lax.broadcasted_iota(jnp.int32, (width, width), 0)
    cols = lax.broadcasted_iota(jnp.int32, (width, width), 1)
    folded = jnp.where(rows <= cols, top_left, low_right)
    count = lax.axis_size("rec")
    padded = -(-(2 * width + 1) // (8 * count)) * 8 * count
    packed = jnp.concatenate(
        [
            folded,
            top_right,
            diagonal_of(low_right)[None, :],
            jnp.zeros((padded - 2 * width - 1, width), jnp.float32),
        ],
        axis=0,
    )
    summed = reduce_over_records(packed)
    folded = summed[:width]
    top_right = summed[width : 2 * width]
    low_diag = summed[2 * width]
    mirrored = folded.T
    top_left = jnp.where(rows <= cols, folded, mirrored)
    low_right = jnp.where(rows > cols, folded, jnp.where(rows < cols, mirrored, low_diag[None, :]))
    return top_left, top_right, top_right.T, low_right


def local(design, record_weight):
    width = design.shape[1] // 2
    weighted = (design.astype(jnp.float32) * record_weight[:, None]).astype(jnp.bfloat16)
    upper_block = weighted[:, :width]
    lower_block = weighted[:, width:]
    position = lax.axis_index("col")
    device_count = lax.axis_size("col")
    for round_index in range(ROUNDS):
        moving = round_index + 1 < ROUNDS
        pair_data = jnp.concatenate([upper_block, lower_block], axis=1)
        rotation = rotation_of(*summed_gram(pair_data, width))
        rotated = jnp.dot(pair_data, rotation, preferred_element_type=jnp.float32).astype(
            jnp.bfloat16
        )
        new_upper = rotated[:, :width]
        new_lower = rotated[:, width:]
        if moving:
            from_right = send_left(new_lower)
            from_left = send_right(jnp.where(position == 0, new_lower, new_upper))
        if moving:
            upper_block = jnp.where(position == 0, new_upper, from_left)
            lower_block = jnp.where(position == device_count - 1, new_upper, from_right)
        else:
            upper_block = new_upper
            lower_block = new_lower
    rotated_design = jnp.concatenate([upper_block, lower_block], axis=1)
    squares = jnp.sum(jnp.square(rotated_design.astype(jnp.float32)), axis=0)
    count = lax.axis_size("rec")
    spread = jnp.broadcast_to(squares[None], (count,) + squares.shape)
    totals = lax.all_to_all(spread, "rec", 0, 0, tiled=False).sum(axis=0)
    record_total = design.shape[0] * lax.axis_size("rec")
    column_rms = jnp.sqrt(totals / record_total + 1e-06)
    return (rotated_design, column_rms)


def solution(mesh):
    placed = (P("rec", "col"), P("rec"))
    return jax.shard_map(
        local, mesh=mesh, in_specs=placed, out_specs=(P("rec", "col"), P("col")), check_vma=False
    )
```

```python
import jax
import jax.numpy as jnp
from jax import lax
from jax.experimental import pallas as pl
from jax.experimental.pallas import tpu as pltpu
from jax.sharding import Mesh, PartitionSpec as P

ROUNDS = 3
SWEEPS = 6


eps_angle = 0.01


COLUMN_AXES = ("x_lo", "z", "core")
GROUP_AXES = ("x_hi", "y_hi")
PAIR_AXIS = "y_lo"
RECORD_AXES = GROUP_AXES + (PAIR_AXIS,)


def from_behind(value, steps):
    count = lax.axis_size(COLUMN_AXES)
    leading, last = (max(0, -steps), min(count, count - steps))
    return lax.ppermute(value, COLUMN_AXES, [(source, source + steps) for source in range(leading, last)])


def with_partner(value):
    return value + lax.ppermute(value, PAIR_AXIS, [(0, 1), (1, 0)])


def diagonal_of(matrix):
    size = matrix.shape[0]
    rows = lax.broadcasted_iota(jnp.int32, (size, size), 0)
    cols = lax.broadcasted_iota(jnp.int32, (size, size), 1)
    return jnp.sum(jnp.where(rows == cols, matrix, 0.0), axis=0)


def half_angle_terms(first_diag, second_diag, coupling):
    spread = second_diag - first_diag
    tangent = (
        2.0
        * coupling
        * spread
        / (
            spread * spread
            + 4.0 * coupling * coupling
            + eps_angle * (first_diag + second_diag) ** 2
        )
    )
    double_cos = 1.0 / jnp.sqrt(1.0 + tangent * tangent)
    cosine = jnp.sqrt(0.5 + 0.5 * double_cos)
    sine_value = tangent * double_cos / (2.0 * cosine)
    return cosine, sine_value


def sweeps_kernel(top_left_ref, top_right_ref, low_left_ref, low_right_ref, rotation_ref):
    width = top_left_ref.shape[0]
    top_left = top_left_ref[...]
    top_right = top_right_ref[...]
    low_left = low_left_ref[...]
    low_right = low_right_ref[...]
    rows = lax.broadcasted_iota(jnp.int32, (width, width), 0)
    cols = lax.broadcasted_iota(jnp.int32, (width, width), 1)
    on_diagonal = rows == cols
    first_top = jnp.where(on_diagonal, 1.0, 0.0).astype(jnp.float32)
    first_low = jnp.zeros((width, width), jnp.float32)
    second_top = jnp.zeros((width, width), jnp.float32)
    second_low = first_top

    def both_diagonals(matrix):
        masked = jnp.where(on_diagonal, matrix, 0.0)
        return jnp.sum(masked, axis=0, keepdims=True), jnp.sum(masked, axis=1, keepdims=True)

    def to_left(matrix, axis):
        return pltpu.roll(matrix, width - 1, axis)

    for sweep_index in range(SWEEPS):
        if sweep_index > 0:
            top_right = to_left(top_right, 1)
            low_left = to_left(low_left, 0)
            low_right = to_left(to_left(low_right, 0), 1)
            second_top = to_left(second_top, 1)
            second_low = to_left(second_low, 1)
        first_r, first_c = both_diagonals(top_left)
        second_r, second_c = both_diagonals(low_right)
        coupling_r, coupling_c = both_diagonals(top_right)
        cos_col, sin_col = half_angle_terms(first_r, second_r, coupling_r)
        cos_row, sin_row = half_angle_terms(first_c, second_c, coupling_c)
        left_a = top_left * cos_col - top_right * sin_col
        right_a = top_left * sin_col + top_right * cos_col
        left_b = low_left * cos_col - low_right * sin_col
        right_b = low_left * sin_col + low_right * cos_col
        top_left = cos_row * left_a - sin_row * left_b
        low_left = sin_row * left_a + cos_row * left_b
        top_right = cos_row * right_a - sin_row * right_b
        low_right = sin_row * right_a + cos_row * right_b
        first_top, second_top = (
            first_top * cos_col - second_top * sin_col,
            first_top * sin_col + second_top * cos_col,
        )
        first_low, second_low = (
            first_low * cos_col - second_low * sin_col,
            first_low * sin_col + second_low * cos_col,
        )
    second_top = pltpu.roll(second_top, SWEEPS - 1, 1)
    second_low = pltpu.roll(second_low, SWEEPS - 1, 1)
    out = rotation_ref.dtype
    rotation_ref[:width, :width] = first_top.astype(out)
    rotation_ref[width:, :width] = first_low.astype(out)
    rotation_ref[:width, width:] = second_top.astype(out)
    rotation_ref[width:, width:] = second_low.astype(out)


def rotation_of(top_left, top_right, low_left, low_right):
    width = top_left.shape[0]
    vmem = pl.BlockSpec(memory_space=pltpu.VMEM)
    return pl.pallas_call(
        sweeps_kernel,
        out_shape=jax.ShapeDtypeStruct((2 * width, 2 * width), jnp.bfloat16),
        in_specs=[vmem] * 4,
        out_specs=vmem,
        cost_estimate=pl.CostEstimate(
            flops=SWEEPS * 40 * width * width, transcendentals=SWEEPS * 8 * width, bytes_accessed=5 * 4 * width * width
        ),
    )(top_left, top_right, low_left, low_right)


def send_right(block):
    return from_behind(block, 1)


def send_left(block):
    return from_behind(block, -1)


def inner_products(left_part, right_part):
    return lax.dot_general(
        left_part, right_part, (((0,), (0,)), ((), ())), preferred_element_type=jnp.float32
    )


def gathered_records(block):
    count = lax.axis_size(GROUP_AXES)
    spread = jnp.broadcast_to(block[None], (count,) + block.shape)
    gathered = lax.all_to_all(spread, GROUP_AXES, 0, 0, tiled=False)
    return gathered.reshape(count * block.shape[0], block.shape[1])


def summed_gram(pair_data, width):
    gram_local = inner_products(pair_data, pair_data)
    top_left = gram_local[:width, :width]
    top_right = gram_local[:width, width:]
    low_right = gram_local[width:, width:]
    rows = lax.broadcasted_iota(jnp.int32, (width, width), 0)
    cols = lax.broadcasted_iota(jnp.int32, (width, width), 1)
    folded = jnp.where(rows <= cols, top_left, low_right)
    padded = -(-(2 * width + 1) // 8) * 8
    packed = jnp.concatenate(
        [
            folded,
            top_right,
            diagonal_of(low_right)[None, :],
            jnp.zeros((padded - 2 * width - 1, width), jnp.float32),
        ],
        axis=0,
    )
    summed = with_partner(packed)
    folded = summed[:width]
    top_right = summed[width : 2 * width]
    low_diag = summed[2 * width]
    mirrored = folded.T
    top_left = jnp.where(rows <= cols, folded, mirrored)
    low_right = jnp.where(rows > cols, folded, jnp.where(rows < cols, mirrored, low_diag[None, :]))
    return top_left, top_right, top_right.T, low_right


def local(design, record_weight):
    width = design.shape[1] // 2
    records = design.shape[0]
    weighted = (design.astype(jnp.float32) * record_weight[:, None]).astype(jnp.bfloat16)
    weighted = gathered_records(weighted)
    upper_block = weighted[:, :width]
    lower_block = weighted[:, width:]
    position = lax.axis_index(COLUMN_AXES)
    device_count = lax.axis_size(COLUMN_AXES)
    for round_index in range(ROUNDS):
        moving = round_index + 1 < ROUNDS
        pair_data = jnp.concatenate([upper_block, lower_block], axis=1)
        rotation = rotation_of(*summed_gram(pair_data, width))
        rotated = jnp.dot(pair_data, rotation, preferred_element_type=jnp.float32).astype(
            jnp.bfloat16
        )
        new_upper = rotated[:, :width]
        new_lower = rotated[:, width:]
        if moving:
            from_right = send_left(new_lower)
            from_left = send_right(jnp.where(position == 0, new_lower, new_upper))
        if moving:
            upper_block = jnp.where(position == 0, new_upper, from_left)
            lower_block = jnp.where(position == device_count - 1, new_upper, from_right)
        else:
            upper_block = new_upper
            lower_block = new_lower
    gathered_design = jnp.concatenate([upper_block, lower_block], axis=1)
    squares = with_partner(jnp.sum(jnp.square(gathered_design.astype(jnp.float32)), axis=0))
    record_total = records * lax.axis_size(RECORD_AXES)
    column_rms = jnp.sqrt(squares / record_total + 1e-06)
    start = lax.axis_index(GROUP_AXES) * records
    rotated_design = lax.dynamic_slice_in_dim(gathered_design, start, records, axis=0)
    return (rotated_design, column_rms)


def solution(mesh):
    devices = mesh.devices.reshape(2, mesh.devices.shape[0] // 4, 2, 2, mesh.devices.shape[1] // 4, 2)
    view = Mesh(devices, COLUMN_AXES + RECORD_AXES)
    placed = (P(RECORD_AXES, COLUMN_AXES), P(RECORD_AXES))
    return jax.shard_map(
        local,
        mesh=view,
        in_specs=placed,
        out_specs=(P(RECORD_AXES, COLUMN_AXES), P(COLUMN_AXES)),
        check_vma=False,
    )
```

```python
import jax
import jax.numpy as jnp
from jax import lax
from jax.experimental import pallas as pl
from jax.experimental.pallas import tpu as pltpu
from jax.sharding import Mesh, PartitionSpec as P

ROUNDS = 3
SWEEPS = 6


eps_angle = 0.01


COLUMN_AXES = ("x_lo", "z", "core")
GROUP_AXES = ("x_hi", "y_hi")
PAIR_AXIS = "y_lo"
RECORD_AXES = GROUP_AXES + (PAIR_AXIS,)


def from_behind(value, steps):
    count = lax.axis_size(COLUMN_AXES)
    leading, last = (max(0, -steps), min(count, count - steps))
    return lax.ppermute(value, COLUMN_AXES, [(source, source + steps) for source in range(leading, last)])


def with_partner(value):
    return value + lax.ppermute(value, PAIR_AXIS, [(0, 1), (1, 0)])


def diagonal_of(matrix):
    size = matrix.shape[0]
    rows = lax.broadcasted_iota(jnp.int32, (size, size), 0)
    cols = lax.broadcasted_iota(jnp.int32, (size, size), 1)
    return jnp.sum(jnp.where(rows == cols, matrix, 0.0), axis=0)


def half_angle_terms(first_diag, second_diag, coupling):
    spread = second_diag - first_diag
    tangent = (
        2.0
        * coupling
        * spread
        / (
            spread * spread
            + 4.0 * coupling * coupling
            + eps_angle * (first_diag + second_diag) ** 2
        )
    )
    double_cos = 1.0 / jnp.sqrt(1.0 + tangent * tangent)
    cosine = jnp.sqrt(0.5 + 0.5 * double_cos)
    sine_value = tangent * double_cos / (2.0 * cosine)
    return cosine, sine_value


def sweeps_kernel(top_left_ref, top_right_ref, low_left_ref, low_right_ref, rotation_ref):
    width = top_left_ref.shape[0]
    top_left = top_left_ref[...]
    top_right = top_right_ref[...]
    low_left = low_left_ref[...]
    low_right = low_right_ref[...]
    rows = lax.broadcasted_iota(jnp.int32, (width, width), 0)
    cols = lax.broadcasted_iota(jnp.int32, (width, width), 1)
    on_diagonal = rows == cols
    first_top = jnp.where(on_diagonal, 1.0, 0.0).astype(jnp.float32)
    first_low = jnp.zeros((width, width), jnp.float32)
    second_top = jnp.zeros((width, width), jnp.float32)
    second_low = first_top

    def both_diagonals(matrix):
        masked = jnp.where(on_diagonal, matrix, 0.0)
        return jnp.sum(masked, axis=0, keepdims=True), jnp.sum(masked, axis=1, keepdims=True)

    def to_left(matrix, axis):
        return pltpu.roll(matrix, width - 1, axis)

    for sweep_index in range(SWEEPS):
        if sweep_index > 0:
            top_right = to_left(top_right, 1)
            low_left = to_left(low_left, 0)
            low_right = to_left(to_left(low_right, 0), 1)
            second_top = to_left(second_top, 1)
            second_low = to_left(second_low, 1)
        first_r, first_c = both_diagonals(top_left)
        second_r, second_c = both_diagonals(low_right)
        coupling_r, coupling_c = both_diagonals(top_right)
        cos_col, sin_col = half_angle_terms(first_r, second_r, coupling_r)
        cos_row, sin_row = half_angle_terms(first_c, second_c, coupling_c)
        left_a = top_left * cos_col - top_right * sin_col
        right_a = top_left * sin_col + top_right * cos_col
        left_b = low_left * cos_col - low_right * sin_col
        right_b = low_left * sin_col + low_right * cos_col
        top_left = cos_row * left_a - sin_row * left_b
        low_left = sin_row * left_a + cos_row * left_b
        top_right = cos_row * right_a - sin_row * right_b
        low_right = sin_row * right_a + cos_row * right_b
        first_top, second_top = (
            first_top * cos_col - second_top * sin_col,
            first_top * sin_col + second_top * cos_col,
        )
        first_low, second_low = (
            first_low * cos_col - second_low * sin_col,
            first_low * sin_col + second_low * cos_col,
        )
    second_top = pltpu.roll(second_top, SWEEPS - 1, 1)
    second_low = pltpu.roll(second_low, SWEEPS - 1, 1)
    out = rotation_ref.dtype
    rotation_ref[:width, :width] = first_top.astype(out)
    rotation_ref[width:, :width] = first_low.astype(out)
    rotation_ref[:width, width:] = second_top.astype(out)
    rotation_ref[width:, width:] = second_low.astype(out)


def rotation_of(top_left, top_right, low_left, low_right):
    width = top_left.shape[0]
    vmem = pl.BlockSpec(memory_space=pltpu.VMEM)
    return pl.pallas_call(
        sweeps_kernel,
        out_shape=jax.ShapeDtypeStruct((2 * width, 2 * width), jnp.bfloat16),
        in_specs=[vmem] * 4,
        out_specs=vmem,
        cost_estimate=pl.CostEstimate(
            flops=SWEEPS * 40 * width * width, transcendentals=SWEEPS * 8 * width, bytes_accessed=5 * 4 * width * width
        ),
    )(top_left, top_right, low_left, low_right)


def send_right(block):
    return from_behind(block, 1)


def send_left(block):
    return from_behind(block, -1)


def inner_products(left_part, right_part):
    return lax.dot_general(
        left_part, right_part, (((0,), (0,)), ((), ())), preferred_element_type=jnp.float32
    )


def gathered_records(block):
    count = lax.axis_size(GROUP_AXES)
    spread = jnp.broadcast_to(block[None], (count,) + block.shape)
    gathered = lax.all_to_all(spread, GROUP_AXES, 0, 0, tiled=False)
    return gathered.reshape(count * block.shape[0], block.shape[1])


def summed_gram(pair_data, width):
    gram_local = inner_products(pair_data, pair_data)
    top_left = gram_local[:width, :width]
    top_right = gram_local[:width, width:]
    low_right = gram_local[width:, width:]
    rows = lax.broadcasted_iota(jnp.int32, (width, width), 0)
    cols = lax.broadcasted_iota(jnp.int32, (width, width), 1)
    folded = jnp.where(rows <= cols, top_left, low_right)
    padded = -(-(2 * width + 1) // 8) * 8
    packed = jnp.concatenate(
        [
            folded,
            top_right,
            diagonal_of(low_right)[None, :],
            jnp.zeros((padded - 2 * width - 1, width), jnp.float32),
        ],
        axis=0,
    )
    summed = with_partner(packed)
    folded = summed[:width]
    top_right = summed[width : 2 * width]
    low_diag = summed[2 * width]
    mirrored = folded.T
    top_left = jnp.where(rows <= cols, folded, mirrored)
    low_right = jnp.where(rows > cols, folded, jnp.where(rows < cols, mirrored, low_diag[None, :]))
    return top_left, top_right, top_right.T, low_right


def local(design, record_weight):
    width = design.shape[1] // 2
    records = design.shape[0]
    weighted = (design.astype(jnp.float32) * record_weight[:, None]).astype(jnp.bfloat16)
    weighted = gathered_records(weighted)
    upper_block = weighted[:, :width]
    lower_block = weighted[:, width:]
    position = lax.axis_index(COLUMN_AXES)
    device_count = lax.axis_size(COLUMN_AXES)
    for round_index in range(ROUNDS):
        moving = round_index + 1 < ROUNDS
        pair_data = jnp.concatenate([upper_block, lower_block], axis=1)
        if moving:
            pair_from_left = send_right(pair_data)
            pair_from_right = send_left(pair_data)
        rotation = rotation_of(*summed_gram(pair_data, width))
        if not moving:
            rotated = jnp.dot(pair_data, rotation, preferred_element_type=jnp.float32)
            upper_block = rotated[:, :width].astype(jnp.bfloat16)
            lower_block = rotated[:, width:].astype(jnp.bfloat16)
            break
        first_columns = rotation[:, :width]
        second_columns = rotation[:, width:]
        kept = jnp.dot(pair_data, first_columns, preferred_element_type=jnp.float32).astype(jnp.bfloat16)
        columns_from_left = send_right(jnp.where(position == 0, second_columns, first_columns))
        columns_from_right = send_left(second_columns)
        arriving_upper = jnp.dot(
            pair_from_left, columns_from_left, preferred_element_type=jnp.float32
        ).astype(jnp.bfloat16)
        arriving_lower = jnp.dot(
            pair_from_right, columns_from_right, preferred_element_type=jnp.float32
        ).astype(jnp.bfloat16)
        upper_block = jnp.where(position == 0, kept, arriving_upper)
        lower_block = jnp.where(position == device_count - 1, kept, arriving_lower)
    gathered_design = jnp.concatenate([upper_block, lower_block], axis=1)
    squares = with_partner(jnp.sum(jnp.square(gathered_design.astype(jnp.float32)), axis=0))
    record_total = records * lax.axis_size(RECORD_AXES)
    column_rms = jnp.sqrt(squares / record_total + 1e-06)
    start = lax.axis_index(GROUP_AXES) * records
    rotated_design = lax.dynamic_slice_in_dim(gathered_design, start, records, axis=0)
    return (rotated_design, column_rms)


def solution(mesh):
    devices = mesh.devices.reshape(2, mesh.devices.shape[0] // 4, 2, 2, mesh.devices.shape[1] // 4, 2)
    view = Mesh(devices, COLUMN_AXES + RECORD_AXES)
    placed = (P(RECORD_AXES, COLUMN_AXES), P(RECORD_AXES))
    return jax.shard_map(
        local,
        mesh=view,
        in_specs=placed,
        out_specs=(P(RECORD_AXES, COLUMN_AXES), P(COLUMN_AXES)),
        check_vma=False,
    )
```

```python
import jax
import jax.numpy as jnp
from jax import lax
from jax.experimental import pallas as pl
from jax.experimental.pallas import tpu as pltpu
from jax.sharding import Mesh, PartitionSpec as P

ROUNDS = 3
SWEEPS = 6


eps_angle = 0.01


COLUMN_AXES = ("x_lo", "z", "core")
GROUP_AXES = ("x_hi", "y_hi")
PAIR_AXIS = "y_lo"
RECORD_AXES = GROUP_AXES + (PAIR_AXIS,)


def from_behind(value, steps):
    count = lax.axis_size(COLUMN_AXES)
    leading, last = (max(0, -steps), min(count, count - steps))
    return lax.ppermute(value, COLUMN_AXES, [(source, source + steps) for source in range(leading, last)])


def with_partner(value):
    return value + lax.ppermute(value, PAIR_AXIS, [(0, 1), (1, 0)])


def diagonal_of(matrix):
    size = matrix.shape[0]
    rows = lax.broadcasted_iota(jnp.int32, (size, size), 0)
    cols = lax.broadcasted_iota(jnp.int32, (size, size), 1)
    return jnp.sum(jnp.where(rows == cols, matrix, 0.0), axis=0)


def half_angle_terms(first_diag, second_diag, coupling):
    spread = second_diag - first_diag
    tangent = (
        2.0
        * coupling
        * spread
        / (
            spread * spread
            + 4.0 * coupling * coupling
            + eps_angle * (first_diag + second_diag) ** 2
        )
    )
    double_cos = 1.0 / jnp.sqrt(1.0 + tangent * tangent)
    cosine = jnp.sqrt(0.5 + 0.5 * double_cos)
    sine_value = tangent * double_cos / (2.0 * cosine)
    return cosine, sine_value


def sweeps_kernel(packed_ref, rotation_ref):
    width = packed_ref.shape[1]
    rows = lax.broadcasted_iota(jnp.int32, (width, width), 0)
    cols = lax.broadcasted_iota(jnp.int32, (width, width), 1)
    on_diagonal = rows == cols
    folded = packed_ref[:width, :]
    top_right = packed_ref[width : 2 * width, :]
    low_diag = packed_ref[2 * width : 2 * width + 8, :][:1, :]
    mirrored = folded.T
    top_left = jnp.where(rows <= cols, folded, mirrored)
    low_right = jnp.where(rows > cols, folded, jnp.where(rows < cols, mirrored, low_diag))
    low_left = top_right.T
    first_top = jnp.where(on_diagonal, 1.0, 0.0).astype(jnp.float32)
    first_low = jnp.zeros((width, width), jnp.float32)
    second_top = jnp.zeros((width, width), jnp.float32)
    second_low = first_top

    def diagonal_row(matrix):
        return jnp.sum(jnp.where(on_diagonal, matrix, 0.0), axis=0, keepdims=True)

    def as_column(row):
        return jnp.broadcast_to(row, (128, width)).T[:, :1]

    def to_left(matrix, axis):
        return pltpu.roll(matrix, width - 1, axis)

    for sweep_index in range(SWEEPS):
        if sweep_index > 0:
            top_right = to_left(top_right, 1)
            low_left = to_left(low_left, 0)
            low_right = to_left(to_left(low_right, 0), 1)
            second_top = to_left(second_top, 1)
            second_low = to_left(second_low, 1)
        cos_col, sin_col = half_angle_terms(
            diagonal_row(top_left), diagonal_row(low_right), diagonal_row(top_right)
        )
        cos_row = as_column(cos_col)
        sin_row = as_column(sin_col)
        left_a = top_left * cos_col - top_right * sin_col
        right_a = top_left * sin_col + top_right * cos_col
        left_b = low_left * cos_col - low_right * sin_col
        right_b = low_left * sin_col + low_right * cos_col
        top_left = cos_row * left_a - sin_row * left_b
        low_left = sin_row * left_a + cos_row * left_b
        top_right = cos_row * right_a - sin_row * right_b
        low_right = sin_row * right_a + cos_row * right_b
        first_top, second_top = (
            first_top * cos_col - second_top * sin_col,
            first_top * sin_col + second_top * cos_col,
        )
        first_low, second_low = (
            first_low * cos_col - second_low * sin_col,
            first_low * sin_col + second_low * cos_col,
        )
    second_top = pltpu.roll(second_top, SWEEPS - 1, 1)
    second_low = pltpu.roll(second_low, SWEEPS - 1, 1)
    out = rotation_ref.dtype
    rotation_ref[:width, :width] = first_top.astype(out)
    rotation_ref[width:, :width] = first_low.astype(out)
    rotation_ref[:width, width:] = second_top.astype(out)
    rotation_ref[width:, width:] = second_low.astype(out)


def rotation_of(packed):
    width = packed.shape[1]
    vmem = pl.BlockSpec(memory_space=pltpu.VMEM)
    return pl.pallas_call(
        sweeps_kernel,
        out_shape=jax.ShapeDtypeStruct((2 * width, 2 * width), jnp.bfloat16),
        in_specs=[vmem],
        out_specs=vmem,
        cost_estimate=pl.CostEstimate(
            flops=SWEEPS * 40 * width * width, transcendentals=SWEEPS * 8 * width, bytes_accessed=4 * 4 * width * width
        ),
    )(packed)


def send_right(block):
    return from_behind(block, 1)


def send_left(block):
    return from_behind(block, -1)


def inner_products(left_part, right_part):
    return lax.dot_general(
        left_part, right_part, (((0,), (0,)), ((), ())), preferred_element_type=jnp.float32
    )


def gathered_records(block):
    count = lax.axis_size(GROUP_AXES)
    spread = jnp.broadcast_to(block[None], (count,) + block.shape)
    gathered = lax.all_to_all(spread, GROUP_AXES, 0, 0, tiled=False)
    return gathered.reshape(count * block.shape[0], block.shape[1])


def summed_gram(pair_data, width):
    gram_local = inner_products(pair_data, pair_data)
    top_left = gram_local[:width, :width]
    top_right = gram_local[:width, width:]
    low_right = gram_local[width:, width:]
    rows = lax.broadcasted_iota(jnp.int32, (width, width), 0)
    cols = lax.broadcasted_iota(jnp.int32, (width, width), 1)
    folded = jnp.where(rows <= cols, top_left, low_right)
    padded = -(-(2 * width + 1) // 8) * 8
    packed = jnp.concatenate(
        [
            folded,
            top_right,
            diagonal_of(low_right)[None, :],
            jnp.zeros((padded - 2 * width - 1, width), jnp.float32),
        ],
        axis=0,
    )
    return with_partner(packed)


def local(design, record_weight):
    width = design.shape[1] // 2
    records = design.shape[0]
    weighted = (design.astype(jnp.float32) * record_weight[:, None]).astype(jnp.bfloat16)
    weighted = gathered_records(weighted)
    upper_block = weighted[:, :width]
    lower_block = weighted[:, width:]
    position = lax.axis_index(COLUMN_AXES)
    device_count = lax.axis_size(COLUMN_AXES)
    for round_index in range(ROUNDS):
        moving = round_index + 1 < ROUNDS
        pair_data = jnp.concatenate([upper_block, lower_block], axis=1)
        rotation = rotation_of(summed_gram(pair_data, width))
        rotated = jnp.dot(pair_data, rotation, preferred_element_type=jnp.float32).astype(
            jnp.bfloat16
        )
        new_upper = rotated[:, :width]
        new_lower = rotated[:, width:]
        if moving:
            from_right = send_left(new_lower)
            from_left = send_right(jnp.where(position == 0, new_lower, new_upper))
        if moving:
            upper_block = jnp.where(position == 0, new_upper, from_left)
            lower_block = jnp.where(position == device_count - 1, new_upper, from_right)
        else:
            upper_block = new_upper
            lower_block = new_lower
    gathered_design = jnp.concatenate([upper_block, lower_block], axis=1)
    squares = with_partner(jnp.sum(jnp.square(gathered_design.astype(jnp.float32)), axis=0))
    record_total = records * lax.axis_size(RECORD_AXES)
    column_rms = jnp.sqrt(squares / record_total + 1e-06)
    start = lax.axis_index(GROUP_AXES) * records
    rotated_design = lax.dynamic_slice_in_dim(gathered_design, start, records, axis=0)
    return (rotated_design, column_rms)


def solution(mesh):
    devices = mesh.devices.reshape(2, mesh.devices.shape[0] // 4, 2, 2, mesh.devices.shape[1] // 4, 2)
    view = Mesh(devices, COLUMN_AXES + RECORD_AXES)
    placed = (P(RECORD_AXES, COLUMN_AXES), P(RECORD_AXES))
    return jax.shard_map(
        local,
        mesh=view,
        in_specs=placed,
        out_specs=(P(RECORD_AXES, COLUMN_AXES), P(COLUMN_AXES)),
        check_vma=False,
    )
```

```python
import jax
import jax.numpy as jnp
from jax import lax
from jax.experimental import pallas as pl
from jax.experimental.pallas import tpu as pltpu
from jax.sharding import Mesh, PartitionSpec as P

ROUNDS = 3
SWEEPS = 6


eps_angle = 0.01


COLUMN_AXES = ("x_lo", "z", "core")
GROUP_AXES = ("x_hi", "y_hi")
PAIR_AXIS = "y_lo"
RECORD_AXES = GROUP_AXES + (PAIR_AXIS,)


def from_behind(value, steps):
    count = lax.axis_size(COLUMN_AXES)
    leading, last = (max(0, -steps), min(count, count - steps))
    return lax.ppermute(value, COLUMN_AXES, [(source, source + steps) for source in range(leading, last)])


PARTNER_AXES = ("core", "y_hi", PAIR_AXIS)


def partner_pairs(halves):
    pairs = []
    for half in range(halves):
        for core, other in ((0, half), (1, (half - 1) % halves)):
            even, odd = (core * halves + half) * 2, (core * halves + other) * 2 + 1
            pairs += [(even, odd), (odd, even)]
    return pairs


def with_partner(value):
    return value + lax.ppermute(value, PARTNER_AXES, partner_pairs(lax.axis_size("y_hi")))


def diagonal_of(matrix):
    size = matrix.shape[0]
    rows = lax.broadcasted_iota(jnp.int32, (size, size), 0)
    cols = lax.broadcasted_iota(jnp.int32, (size, size), 1)
    return jnp.sum(jnp.where(rows == cols, matrix, 0.0), axis=0)


def half_angle_terms(first_diag, second_diag, coupling):
    spread = second_diag - first_diag
    tangent = (
        2.0
        * coupling
        * spread
        / (
            spread * spread
            + 4.0 * coupling * coupling
            + eps_angle * (first_diag + second_diag) ** 2
        )
    )
    double_cos = 1.0 / jnp.sqrt(1.0 + tangent * tangent)
    cosine = jnp.sqrt(0.5 + 0.5 * double_cos)
    sine_value = tangent * double_cos / (2.0 * cosine)
    return cosine, sine_value


def sweeps_kernel(packed_ref, rotation_ref):
    width = packed_ref.shape[1]
    rows = lax.broadcasted_iota(jnp.int32, (width, width), 0)
    cols = lax.broadcasted_iota(jnp.int32, (width, width), 1)
    on_diagonal = rows == cols
    folded = packed_ref[:width, :]
    top_right = packed_ref[width : 2 * width, :]
    low_diag = packed_ref[2 * width : 2 * width + 8, :][:1, :]
    mirrored = folded.T
    top_left = jnp.where(rows <= cols, folded, mirrored)
    low_right = jnp.where(rows > cols, folded, jnp.where(rows < cols, mirrored, low_diag))
    low_left = top_right.T
    first_top = jnp.where(on_diagonal, 1.0, 0.0).astype(jnp.float32)
    first_low = jnp.zeros((width, width), jnp.float32)
    second_top = jnp.zeros((width, width), jnp.float32)
    second_low = first_top

    def diagonal_row(matrix):
        return jnp.sum(jnp.where(on_diagonal, matrix, 0.0), axis=0, keepdims=True)

    def as_column(row):
        return jnp.broadcast_to(row, (128, width)).T[:, :1]

    def to_left(matrix, axis):
        return pltpu.roll(matrix, width - 1, axis)

    for sweep_index in range(SWEEPS):
        if sweep_index > 0:
            top_right = to_left(top_right, 1)
            low_left = to_left(low_left, 0)
            low_right = to_left(to_left(low_right, 0), 1)
            second_top = to_left(second_top, 1)
            second_low = to_left(second_low, 1)
        cos_col, sin_col = half_angle_terms(
            diagonal_row(top_left), diagonal_row(low_right), diagonal_row(top_right)
        )
        cos_row = as_column(cos_col)
        sin_row = as_column(sin_col)
        left_a = top_left * cos_col - top_right * sin_col
        right_a = top_left * sin_col + top_right * cos_col
        left_b = low_left * cos_col - low_right * sin_col
        right_b = low_left * sin_col + low_right * cos_col
        top_left = cos_row * left_a - sin_row * left_b
        low_left = sin_row * left_a + cos_row * left_b
        top_right = cos_row * right_a - sin_row * right_b
        low_right = sin_row * right_a + cos_row * right_b
        first_top, second_top = (
            first_top * cos_col - second_top * sin_col,
            first_top * sin_col + second_top * cos_col,
        )
        first_low, second_low = (
            first_low * cos_col - second_low * sin_col,
            first_low * sin_col + second_low * cos_col,
        )
    second_top = pltpu.roll(second_top, SWEEPS - 1, 1)
    second_low = pltpu.roll(second_low, SWEEPS - 1, 1)
    out = rotation_ref.dtype
    rotation_ref[:width, :width] = first_top.astype(out)
    rotation_ref[width:, :width] = first_low.astype(out)
    rotation_ref[:width, width:] = second_top.astype(out)
    rotation_ref[width:, width:] = second_low.astype(out)


def rotation_of(packed):
    width = packed.shape[1]
    vmem = pl.BlockSpec(memory_space=pltpu.VMEM)
    return pl.pallas_call(
        sweeps_kernel,
        out_shape=jax.ShapeDtypeStruct((2 * width, 2 * width), jnp.bfloat16),
        in_specs=[vmem],
        out_specs=vmem,
        cost_estimate=pl.CostEstimate(
            flops=SWEEPS * 40 * width * width, transcendentals=SWEEPS * 8 * width, bytes_accessed=4 * 4 * width * width
        ),
    )(packed)


def send_right(block):
    return from_behind(block, 1)


def send_left(block):
    return from_behind(block, -1)


def inner_products(left_part, right_part):
    return lax.dot_general(
        left_part, right_part, (((0,), (0,)), ((), ())), preferred_element_type=jnp.float32
    )


def gathered_records(block):
    count = lax.axis_size(GROUP_AXES)
    spread = jnp.broadcast_to(block[None], (count,) + block.shape)
    gathered = lax.all_to_all(spread, GROUP_AXES, 0, 0, tiled=False)
    return gathered.reshape(count * block.shape[0], block.shape[1])


def summed_gram(pair_data, width):
    gram_local = inner_products(pair_data, pair_data)
    top_left = gram_local[:width, :width]
    top_right = gram_local[:width, width:]
    low_right = gram_local[width:, width:]
    rows = lax.broadcasted_iota(jnp.int32, (width, width), 0)
    cols = lax.broadcasted_iota(jnp.int32, (width, width), 1)
    folded = jnp.where(rows <= cols, top_left, low_right)
    padded = -(-(2 * width + 1) // 8) * 8
    packed = jnp.concatenate(
        [
            folded,
            top_right,
            diagonal_of(low_right)[None, :],
            jnp.zeros((padded - 2 * width - 1, width), jnp.float32),
        ],
        axis=0,
    )
    return with_partner(packed)


def local(design, record_weight):
    width = design.shape[1] // 2
    records = design.shape[0]
    weighted = (design.astype(jnp.float32) * record_weight[:, None]).astype(jnp.bfloat16)
    weighted = gathered_records(weighted)
    upper_block = weighted[:, :width]
    lower_block = weighted[:, width:]
    position = lax.axis_index(COLUMN_AXES)
    device_count = lax.axis_size(COLUMN_AXES)
    for round_index in range(ROUNDS):
        moving = round_index + 1 < ROUNDS
        pair_data = jnp.concatenate([upper_block, lower_block], axis=1)
        rotation = rotation_of(summed_gram(pair_data, width))
        rotated = jnp.dot(pair_data, rotation, preferred_element_type=jnp.float32).astype(
            jnp.bfloat16
        )
        new_upper = rotated[:, :width]
        new_lower = rotated[:, width:]
        if moving:
            from_right = send_left(new_lower)
            from_left = send_right(jnp.where(position == 0, new_lower, new_upper))
        if moving:
            upper_block = jnp.where(position == 0, new_upper, from_left)
            lower_block = jnp.where(position == device_count - 1, new_upper, from_right)
        else:
            upper_block = new_upper
            lower_block = new_lower
    gathered_design = jnp.concatenate([upper_block, lower_block], axis=1)
    squares = with_partner(jnp.sum(jnp.square(gathered_design.astype(jnp.float32)), axis=0))
    record_total = records * lax.axis_size(RECORD_AXES)
    column_rms = jnp.sqrt(squares / record_total + 1e-06)
    start = lax.axis_index(GROUP_AXES) * records
    rotated_design = lax.dynamic_slice_in_dim(gathered_design, start, records, axis=0)
    return (rotated_design, column_rms)


def solution(mesh):
    devices = mesh.devices.reshape(2, mesh.devices.shape[0] // 4, 2, 2, mesh.devices.shape[1] // 4, 2)
    view = Mesh(devices, COLUMN_AXES + RECORD_AXES)
    placed = (P(RECORD_AXES, COLUMN_AXES), P(RECORD_AXES))
    return jax.shard_map(
        local,
        mesh=view,
        in_specs=placed,
        out_specs=(P(RECORD_AXES, COLUMN_AXES), P(COLUMN_AXES)),
        check_vma=False,
    )
```

```python
import jax
import jax.numpy as jnp
from jax import lax
from jax.experimental import pallas as pl
from jax.experimental.pallas import tpu as pltpu
from jax.sharding import Mesh, PartitionSpec as P

ROUNDS = 3
SWEEPS = 6


eps_angle = 0.01


COLUMN_AXES = ("x_lo", "z", "core")
GROUP_AXES = ("x_hi", "y_hi")
PAIR_AXIS = "y_lo"
RECORD_AXES = GROUP_AXES + (PAIR_AXIS,)


def from_behind(value, steps):
    count = lax.axis_size(COLUMN_AXES)
    leading, last = (max(0, -steps), min(count, count - steps))
    return lax.ppermute(value, COLUMN_AXES, [(source, source + steps) for source in range(leading, last)])


PARTNER_AXES = ("core", "y_hi", PAIR_AXIS)


def partner_pairs(halves):
    pairs = []
    for half in range(halves):
        for core, other in ((0, half), (1, (half - 1) % halves)):
            even, odd = (core * halves + half) * 2, (core * halves + other) * 2 + 1
            pairs += [(even, odd), (odd, even)]
    return pairs


def with_partner(value):
    return value + lax.ppermute(value, PARTNER_AXES, partner_pairs(lax.axis_size("y_hi")))


def diagonal_of(matrix):
    size = matrix.shape[0]
    rows = lax.broadcasted_iota(jnp.int32, (size, size), 0)
    cols = lax.broadcasted_iota(jnp.int32, (size, size), 1)
    return jnp.sum(jnp.where(rows == cols, matrix, 0.0), axis=0)


def half_angle_terms(first_diag, second_diag, coupling):
    spread = second_diag - first_diag
    tangent = (
        2.0
        * coupling
        * spread
        / (
            spread * spread
            + 4.0 * coupling * coupling
            + eps_angle * (first_diag + second_diag) ** 2
        )
    )
    double_cos = 1.0 / jnp.sqrt(1.0 + tangent * tangent)
    cosine = jnp.sqrt(0.5 + 0.5 * double_cos)
    sine_value = tangent * double_cos / (2.0 * cosine)
    return cosine, sine_value


def sweeps_kernel(packed_ref, rotation_ref):
    width = packed_ref.shape[1]
    rows = lax.broadcasted_iota(jnp.int32, (width, width), 0)
    cols = lax.broadcasted_iota(jnp.int32, (width, width), 1)
    on_diagonal = rows == cols
    folded = packed_ref[:width, :]
    top_right = packed_ref[width : 2 * width, :]
    low_diag = packed_ref[2 * width : 2 * width + 8, :][:1, :]
    mirrored = folded.T
    top_left = jnp.where(rows <= cols, folded, mirrored)
    low_right = jnp.where(rows > cols, folded, jnp.where(rows < cols, mirrored, low_diag))
    low_left = top_right.T
    first_top = jnp.where(on_diagonal, 1.0, 0.0).astype(jnp.float32)
    first_low = jnp.zeros((width, width), jnp.float32)
    second_top = jnp.zeros((width, width), jnp.float32)
    second_low = first_top

    def diagonal_row(matrix):
        return jnp.sum(jnp.where(on_diagonal, matrix, 0.0), axis=0, keepdims=True)

    def as_column(row):
        return jnp.broadcast_to(row, (128, width)).T[:, :1]

    def to_left(matrix, axis):
        return pltpu.roll(matrix, width - 1, axis)

    for sweep_index in range(SWEEPS):
        if sweep_index > 0:
            top_right = to_left(top_right, 1)
            low_left = to_left(low_left, 0)
            low_right = to_left(to_left(low_right, 0), 1)
            second_top = to_left(second_top, 1)
            second_low = to_left(second_low, 1)
        cos_col, sin_col = half_angle_terms(
            diagonal_row(top_left), diagonal_row(low_right), diagonal_row(top_right)
        )
        cos_row = as_column(cos_col)
        sin_row = as_column(sin_col)
        left_a = top_left * cos_col - top_right * sin_col
        right_a = top_left * sin_col + top_right * cos_col
        left_b = low_left * cos_col - low_right * sin_col
        right_b = low_left * sin_col + low_right * cos_col
        top_left = cos_row * left_a - sin_row * left_b
        low_left = sin_row * left_a + cos_row * left_b
        top_right = cos_row * right_a - sin_row * right_b
        low_right = sin_row * right_a + cos_row * right_b
        first_top, second_top = (
            first_top * cos_col - second_top * sin_col,
            first_top * sin_col + second_top * cos_col,
        )
        first_low, second_low = (
            first_low * cos_col - second_low * sin_col,
            first_low * sin_col + second_low * cos_col,
        )
    second_top = pltpu.roll(second_top, SWEEPS - 1, 1)
    second_low = pltpu.roll(second_low, SWEEPS - 1, 1)
    out = rotation_ref.dtype
    rotation_ref[:width, :width] = first_top.astype(out)
    rotation_ref[width:, :width] = first_low.astype(out)
    rotation_ref[:width, width:] = second_top.astype(out)
    rotation_ref[width:, width:] = second_low.astype(out)


def rotation_of(packed):
    width = packed.shape[1]
    vmem = pl.BlockSpec(memory_space=pltpu.VMEM)
    return pl.pallas_call(
        sweeps_kernel,
        out_shape=jax.ShapeDtypeStruct((2 * width, 2 * width), jnp.bfloat16),
        in_specs=[vmem],
        out_specs=vmem,
        cost_estimate=pl.CostEstimate(
            flops=SWEEPS * 40 * width * width, transcendentals=SWEEPS * 8 * width, bytes_accessed=4 * 4 * width * width
        ),
    )(packed)


def send_right(block):
    return from_behind(block, 1)


def send_left(block):
    return from_behind(block, -1)


def inner_products(left_part, right_part):
    return lax.dot_general(
        left_part, right_part, (((0,), (0,)), ((), ())), preferred_element_type=jnp.float32
    )


def gathered_records(block):
    count = lax.axis_size(GROUP_AXES)
    spread = jnp.broadcast_to(block[None], (count,) + block.shape)
    gathered = lax.all_to_all(spread, GROUP_AXES, 0, 0, tiled=False)
    return gathered.reshape(count * block.shape[0], block.shape[1])


def summed_gram(pair_data, width):
    gram_local = inner_products(pair_data, pair_data)
    top_left = gram_local[:width, :width]
    top_right = gram_local[:width, width:]
    low_right = gram_local[width:, width:]
    rows = lax.broadcasted_iota(jnp.int32, (width, width), 0)
    cols = lax.broadcasted_iota(jnp.int32, (width, width), 1)
    folded = jnp.where(rows <= cols, top_left, low_right)
    padded = -(-(2 * width + 1) // 8) * 8
    packed = jnp.concatenate(
        [
            folded,
            top_right,
            diagonal_of(low_right)[None, :],
            jnp.zeros((padded - 2 * width - 1, width), jnp.float32),
        ],
        axis=0,
    )
    return with_partner(packed)


def local(design, record_weight):
    width = design.shape[1] // 2
    records = design.shape[0]
    weighted = (design.astype(jnp.float32) * record_weight[:, None]).astype(jnp.bfloat16)
    weighted = gathered_records(weighted)
    upper_block = weighted[:, :width]
    lower_block = weighted[:, width:]
    position = lax.axis_index(COLUMN_AXES)
    device_count = lax.axis_size(COLUMN_AXES)
    for round_index in range(ROUNDS):
        moving = round_index + 1 < ROUNDS
        pair_data = jnp.concatenate([upper_block, lower_block], axis=1)
        rotation = rotation_of(summed_gram(pair_data, width))
        if not moving:
            rotated = jnp.dot(pair_data, rotation, preferred_element_type=jnp.float32)
            upper_block = rotated[:, :width].astype(jnp.bfloat16)
            lower_block = rotated[:, width:].astype(jnp.bfloat16)
            break
        first_columns = rotation[:, :width]
        second_columns = rotation[:, width:]
        going_right = jnp.dot(
            pair_data,
            jnp.where(position == 0, second_columns, first_columns),
            preferred_element_type=jnp.float32,
        ).astype(jnp.bfloat16)
        going_left = jnp.dot(
            pair_data,
            jnp.where(position == 0, first_columns, second_columns),
            preferred_element_type=jnp.float32,
        ).astype(jnp.bfloat16)
        from_left = send_right(going_right)
        from_right = send_left(going_left)
        upper_block = jnp.where(position == 0, going_left, from_left)
        lower_block = jnp.where(position == device_count - 1, going_right, from_right)
    gathered_design = jnp.concatenate([upper_block, lower_block], axis=1)
    squares = with_partner(jnp.sum(jnp.square(gathered_design.astype(jnp.float32)), axis=0))
    record_total = records * lax.axis_size(RECORD_AXES)
    column_rms = jnp.sqrt(squares / record_total + 1e-06)
    start = lax.axis_index(GROUP_AXES) * records
    rotated_design = lax.dynamic_slice_in_dim(gathered_design, start, records, axis=0)
    return (rotated_design, column_rms)


def solution(mesh):
    devices = mesh.devices.reshape(2, mesh.devices.shape[0] // 4, 2, 2, mesh.devices.shape[1] // 4, 2)
    view = Mesh(devices, COLUMN_AXES + RECORD_AXES)
    placed = (P(RECORD_AXES, COLUMN_AXES), P(RECORD_AXES))
    return jax.shard_map(
        local,
        mesh=view,
        in_specs=placed,
        out_specs=(P(RECORD_AXES, COLUMN_AXES), P(COLUMN_AXES)),
        check_vma=False,
    )
```

```python
import jax
import jax.numpy as jnp
from jax import lax
from jax.experimental import pallas as pl
from jax.experimental.pallas import tpu as pltpu
from jax.sharding import Mesh, PartitionSpec as P

ROUNDS = 3
SWEEPS = 6


eps_angle = 0.01


COLUMN_AXES = ("x_lo", "z", "core")
GROUP_AXES = ("x_hi", "y_hi")
PAIR_AXIS = "y_lo"
RECORD_AXES = GROUP_AXES + (PAIR_AXIS,)


def from_behind(value, steps):
    count = lax.axis_size(COLUMN_AXES)
    leading, last = (max(0, -steps), min(count, count - steps))
    return lax.ppermute(value, COLUMN_AXES, [(source, source + steps) for source in range(leading, last)])


PARTNER_AXES = ("core", "y_hi", PAIR_AXIS)


def partner_pairs(halves):
    pairs = []
    for half in range(halves):
        for core, other in ((0, half), (1, (half - 1) % halves)):
            even, odd = (core * halves + half) * 2, (core * halves + other) * 2 + 1
            pairs += [(even, odd), (odd, even)]
    return pairs


def with_partner(value):
    return value + lax.ppermute(value, PARTNER_AXES, partner_pairs(lax.axis_size("y_hi")))


def diagonal_of(matrix):
    size = matrix.shape[0]
    rows = lax.broadcasted_iota(jnp.int32, (size, size), 0)
    cols = lax.broadcasted_iota(jnp.int32, (size, size), 1)
    return jnp.sum(jnp.where(rows == cols, matrix, 0.0), axis=0)


def half_angle_terms(first_diag, second_diag, coupling):
    spread = second_diag - first_diag
    tangent = (
        2.0
        * coupling
        * spread
        / (
            spread * spread
            + 4.0 * coupling * coupling
            + eps_angle * (first_diag + second_diag) ** 2
        )
    )
    double_cos = 1.0 / jnp.sqrt(1.0 + tangent * tangent)
    cosine = jnp.sqrt(0.5 + 0.5 * double_cos)
    sine_value = tangent * double_cos / (2.0 * cosine)
    return cosine, sine_value


def sweeps_kernel(packed_ref, rotation_ref):
    width = packed_ref.shape[1]
    rows = lax.broadcasted_iota(jnp.int32, (width, width), 0)
    cols = lax.broadcasted_iota(jnp.int32, (width, width), 1)
    on_diagonal = rows == cols
    folded = packed_ref[:width, :]
    top_right = packed_ref[width : 2 * width, :]
    low_diag = packed_ref[2 * width : 2 * width + 8, :][:1, :]
    mirrored = folded.T
    top_left = jnp.where(rows <= cols, folded, mirrored)
    low_right = jnp.where(rows > cols, folded, jnp.where(rows < cols, mirrored, low_diag))
    low_left = top_right.T
    first_top = jnp.where(on_diagonal, 1.0, 0.0).astype(jnp.float32)
    first_low = jnp.zeros((width, width), jnp.float32)
    second_top = jnp.zeros((width, width), jnp.float32)
    second_low = first_top

    def diagonal_row(matrix):
        return jnp.sum(jnp.where(on_diagonal, matrix, 0.0), axis=0, keepdims=True)

    def as_column(row):
        return jnp.broadcast_to(row, (128, width)).T[:, :1]

    def to_left(matrix, axis):
        return pltpu.roll(matrix, width - 1, axis)

    for sweep_index in range(SWEEPS):
        if sweep_index > 0:
            top_right = to_left(top_right, 1)
            low_left = to_left(low_left, 0)
            low_right = to_left(to_left(low_right, 0), 1)
            second_top = to_left(second_top, 1)
            second_low = to_left(second_low, 1)
        cos_col, sin_col = half_angle_terms(
            diagonal_row(top_left), diagonal_row(low_right), diagonal_row(top_right)
        )
        cos_row = as_column(cos_col)
        sin_row = as_column(sin_col)
        left_a = top_left * cos_col - top_right * sin_col
        right_a = top_left * sin_col + top_right * cos_col
        left_b = low_left * cos_col - low_right * sin_col
        right_b = low_left * sin_col + low_right * cos_col
        top_left = cos_row * left_a - sin_row * left_b
        low_left = sin_row * left_a + cos_row * left_b
        top_right = cos_row * right_a - sin_row * right_b
        low_right = sin_row * right_a + cos_row * right_b
        first_top, second_top = (
            first_top * cos_col - second_top * sin_col,
            first_top * sin_col + second_top * cos_col,
        )
        first_low, second_low = (
            first_low * cos_col - second_low * sin_col,
            first_low * sin_col + second_low * cos_col,
        )
    second_top = pltpu.roll(second_top, SWEEPS - 1, 1)
    second_low = pltpu.roll(second_low, SWEEPS - 1, 1)
    out = rotation_ref.dtype
    rotation_ref[:width, :width] = first_top.astype(out)
    rotation_ref[width:, :width] = first_low.astype(out)
    rotation_ref[:width, width:] = second_top.astype(out)
    rotation_ref[width:, width:] = second_low.astype(out)


def rotation_of(packed):
    width = packed.shape[1]
    vmem = pl.BlockSpec(memory_space=pltpu.VMEM)
    return pl.pallas_call(
        sweeps_kernel,
        out_shape=jax.ShapeDtypeStruct((2 * width, 2 * width), jnp.bfloat16),
        in_specs=[vmem],
        out_specs=vmem,
        cost_estimate=pl.CostEstimate(
            flops=SWEEPS * 40 * width * width, transcendentals=SWEEPS * 8 * width, bytes_accessed=4 * 4 * width * width
        ),
    )(packed)


def send_right(block):
    return from_behind(block, 1)


def send_left(block):
    return from_behind(block, -1)


def inner_products(left_part, right_part):
    return lax.dot_general(
        left_part, right_part, (((0,), (0,)), ((), ())), preferred_element_type=jnp.float32
    )


def gathered_records(block):
    count = lax.axis_size(GROUP_AXES)
    spread = jnp.broadcast_to(block[None], (count,) + block.shape)
    gathered = lax.all_to_all(spread, GROUP_AXES, 0, 0, tiled=False)
    return gathered.reshape(count * block.shape[0], block.shape[1])


def summed_gram(pair_data, width):
    gram_local = inner_products(pair_data, pair_data)
    top_left = gram_local[:width, :width]
    top_right = gram_local[:width, width:]
    low_right = gram_local[width:, width:]
    rows = lax.broadcasted_iota(jnp.int32, (width, width), 0)
    cols = lax.broadcasted_iota(jnp.int32, (width, width), 1)
    folded = jnp.where(rows <= cols, top_left, low_right)
    padded = -(-(2 * width + 1) // 8) * 8
    packed = jnp.concatenate(
        [
            folded,
            top_right,
            diagonal_of(low_right)[None, :],
            jnp.zeros((padded - 2 * width - 1, width), jnp.float32),
        ],
        axis=0,
    )
    return with_partner(packed)


def local(design, record_weight):
    width = design.shape[1] // 2
    records = design.shape[0]
    weighted = (design.astype(jnp.float32) * record_weight[:, None]).astype(jnp.bfloat16)
    weighted = gathered_records(weighted)
    upper_block = weighted[:, :width]
    lower_block = weighted[:, width:]
    position = lax.axis_index(COLUMN_AXES)
    device_count = lax.axis_size(COLUMN_AXES)
    core = lax.axis_index("core")
    across_pairs = [(k, k + 1) for k in range(1, device_count - 1, 2)] + [
        (k, k - 1) for k in range(2, device_count, 2)
    ]
    for round_index in range(ROUNDS):
        moving = round_index + 1 < ROUNDS
        pair_data = jnp.concatenate([upper_block, lower_block], axis=1)
        rotation = rotation_of(summed_gram(pair_data, width))
        if not moving:
            rotated = jnp.dot(pair_data, rotation, preferred_element_type=jnp.float32)
            upper_block = rotated[:, :width].astype(jnp.bfloat16)
            lower_block = rotated[:, width:].astype(jnp.bfloat16)
            break
        first_columns = rotation[:, :width]
        second_columns = rotation[:, width:]
        right_columns = jnp.where(position == 0, second_columns, first_columns)
        left_columns = jnp.where(position == 0, first_columns, second_columns)
        core_zero = core == 0
        within = jnp.dot(
            pair_data,
            jnp.where(core_zero, right_columns, left_columns),
            preferred_element_type=jnp.float32,
        ).astype(jnp.bfloat16)
        across = jnp.dot(
            pair_data,
            jnp.where(core_zero, left_columns, right_columns),
            preferred_element_type=jnp.float32,
        ).astype(jnp.bfloat16)
        within_in = lax.ppermute(within, "core", [(0, 1), (1, 0)])
        across_in = lax.ppermute(across, COLUMN_AXES, across_pairs)
        upper_block = jnp.where(position == 0, across, jnp.where(core_zero, across_in, within_in))
        lower_block = jnp.where(
            position == device_count - 1, across, jnp.where(core_zero, within_in, across_in)
        )
    gathered_design = jnp.concatenate([upper_block, lower_block], axis=1)
    squares = with_partner(jnp.sum(jnp.square(gathered_design.astype(jnp.float32)), axis=0))
    record_total = records * lax.axis_size(RECORD_AXES)
    column_rms = jnp.sqrt(squares / record_total + 1e-06)
    start = lax.axis_index(GROUP_AXES) * records
    rotated_design = lax.dynamic_slice_in_dim(gathered_design, start, records, axis=0)
    return (rotated_design, column_rms)


def solution(mesh):
    devices = mesh.devices.reshape(2, mesh.devices.shape[0] // 4, 2, 2, mesh.devices.shape[1] // 4, 2)
    view = Mesh(devices, COLUMN_AXES + RECORD_AXES)
    placed = (P(RECORD_AXES, COLUMN_AXES), P(RECORD_AXES))
    return jax.shard_map(
        local,
        mesh=view,
        in_specs=placed,
        out_specs=(P(RECORD_AXES, COLUMN_AXES), P(COLUMN_AXES)),
        check_vma=False,
    )
```

```python
import jax
import jax.numpy as jnp
from jax import lax
from jax.experimental import pallas as pl
from jax.experimental.pallas import tpu as pltpu
from jax.sharding import Mesh, PartitionSpec as P

ROUNDS = 3
SWEEPS = 6


eps_angle = 0.01


COLUMN_AXES = ("x_lo", "z", "core")
GROUP_AXES = ("x_hi", "y_hi")
PAIR_AXIS = "y_lo"
RECORD_AXES = GROUP_AXES + (PAIR_AXIS,)


def from_behind(value, steps):
    count = lax.axis_size(COLUMN_AXES)
    leading, last = (max(0, -steps), min(count, count - steps))
    return lax.ppermute(value, COLUMN_AXES, [(source, source + steps) for source in range(leading, last)])


PARTNER_AXES = ("core", "y_hi", PAIR_AXIS)


def partner_pairs(halves):
    pairs = []
    for half in range(halves):
        for core, other in ((0, half), (1, (half - 1) % halves)):
            even, odd = (core * halves + half) * 2, (core * halves + other) * 2 + 1
            pairs += [(even, odd), (odd, even)]
    return pairs


def with_partner(value):
    return value + lax.ppermute(value, PARTNER_AXES, partner_pairs(lax.axis_size("y_hi")))


def diagonal_of(matrix):
    size = matrix.shape[0]
    rows = lax.broadcasted_iota(jnp.int32, (size, size), 0)
    cols = lax.broadcasted_iota(jnp.int32, (size, size), 1)
    return jnp.sum(jnp.where(rows == cols, matrix, 0.0), axis=0)


def half_angle_terms(first_diag, second_diag, coupling):
    spread = second_diag - first_diag
    tangent = (
        2.0
        * coupling
        * spread
        / (
            spread * spread
            + 4.0 * coupling * coupling
            + eps_angle * (first_diag + second_diag) ** 2
        )
    )
    double_cos = 1.0 / jnp.sqrt(1.0 + tangent * tangent)
    cosine = jnp.sqrt(0.5 + 0.5 * double_cos)
    sine_value = tangent * double_cos / (2.0 * cosine)
    return cosine, sine_value


def sweeps_kernel(packed_ref, rotation_ref):
    width = packed_ref.shape[1]
    rows = lax.broadcasted_iota(jnp.int32, (width, width), 0)
    cols = lax.broadcasted_iota(jnp.int32, (width, width), 1)
    on_diagonal = rows == cols
    folded = packed_ref[:width, :]
    top_right = packed_ref[width : 2 * width, :]
    low_diag = packed_ref[2 * width : 2 * width + 8, :][:1, :]
    mirrored = folded.T
    top_left = jnp.where(rows <= cols, folded, mirrored)
    low_right = jnp.where(rows > cols, folded, jnp.where(rows < cols, mirrored, low_diag))
    low_left = top_right.T
    first_top = jnp.where(on_diagonal, 1.0, 0.0).astype(jnp.float32)
    first_low = jnp.zeros((width, width), jnp.float32)
    second_top = jnp.zeros((width, width), jnp.float32)
    second_low = first_top

    def diagonal_row(matrix):
        return jnp.sum(jnp.where(on_diagonal, matrix, 0.0), axis=0, keepdims=True)

    def as_column(row):
        return jnp.broadcast_to(row, (128, width)).T[:, :1]

    def to_left(matrix, axis):
        return pltpu.roll(matrix, width - 1, axis)

    for sweep_index in range(SWEEPS):
        if sweep_index > 0:
            top_right = to_left(top_right, 1)
            low_left = to_left(low_left, 0)
            low_right = to_left(to_left(low_right, 0), 1)
            second_top = to_left(second_top, 1)
            second_low = to_left(second_low, 1)
        cos_col, sin_col = half_angle_terms(
            diagonal_row(top_left), diagonal_row(low_right), diagonal_row(top_right)
        )
        cos_row = as_column(cos_col)
        sin_row = as_column(sin_col)
        left_a = top_left * cos_col - top_right * sin_col
        right_a = top_left * sin_col + top_right * cos_col
        left_b = low_left * cos_col - low_right * sin_col
        right_b = low_left * sin_col + low_right * cos_col
        top_left = cos_row * left_a - sin_row * left_b
        low_left = sin_row * left_a + cos_row * left_b
        top_right = cos_row * right_a - sin_row * right_b
        low_right = sin_row * right_a + cos_row * right_b
        first_top, second_top = (
            first_top * cos_col - second_top * sin_col,
            first_top * sin_col + second_top * cos_col,
        )
        first_low, second_low = (
            first_low * cos_col - second_low * sin_col,
            first_low * sin_col + second_low * cos_col,
        )
    second_top = pltpu.roll(second_top, SWEEPS - 1, 1)
    second_low = pltpu.roll(second_low, SWEEPS - 1, 1)
    out = rotation_ref.dtype
    rotation_ref[:width, :width] = first_top.astype(out)
    rotation_ref[width:, :width] = first_low.astype(out)
    rotation_ref[:width, width:] = second_top.astype(out)
    rotation_ref[width:, width:] = second_low.astype(out)


def rotation_of(packed):
    width = packed.shape[1]
    vmem = pl.BlockSpec(memory_space=pltpu.VMEM)
    return pl.pallas_call(
        sweeps_kernel,
        out_shape=jax.ShapeDtypeStruct((2 * width, 2 * width), jnp.bfloat16),
        in_specs=[vmem],
        out_specs=vmem,
        cost_estimate=pl.CostEstimate(
            flops=SWEEPS * 40 * width * width, transcendentals=SWEEPS * 8 * width, bytes_accessed=4 * 4 * width * width
        ),
    )(packed)


def send_right(block):
    return from_behind(block, 1)


def send_left(block):
    return from_behind(block, -1)


def inner_products(left_part, right_part):
    return lax.dot_general(
        left_part, right_part, (((0,), (0,)), ((), ())), preferred_element_type=jnp.float32
    )


def gathered_records(block):
    count = lax.axis_size(GROUP_AXES)
    spread = jnp.broadcast_to(block[None], (count,) + block.shape)
    gathered = lax.all_to_all(spread, GROUP_AXES, 0, 0, tiled=False)
    return gathered.reshape(count * block.shape[0], block.shape[1])


def summed_gram(pair_data, width):
    gram_local = inner_products(pair_data, pair_data)
    top_left = gram_local[:width, :width]
    top_right = gram_local[:width, width:]
    low_right = gram_local[width:, width:]
    rows = lax.broadcasted_iota(jnp.int32, (width, width), 0)
    cols = lax.broadcasted_iota(jnp.int32, (width, width), 1)
    folded = jnp.where(rows <= cols, top_left, low_right)
    padded = -(-(2 * width + 1) // 8) * 8
    packed = jnp.concatenate(
        [
            folded,
            top_right,
            diagonal_of(low_right)[None, :],
            jnp.zeros((padded - 2 * width - 1, width), jnp.float32),
        ],
        axis=0,
    )
    return with_partner(packed)


def local(design, record_weight):
    width = design.shape[1] // 2
    records = design.shape[0]
    weighted = (design.astype(jnp.float32) * record_weight[:, None]).astype(jnp.bfloat16)
    upper_block = lax.all_gather(weighted[:, :width], GROUP_AXES, axis=0, tiled=True)
    lower_block = gathered_records(weighted[:, width:])
    position = lax.axis_index(COLUMN_AXES)
    device_count = lax.axis_size(COLUMN_AXES)
    for round_index in range(ROUNDS):
        moving = round_index + 1 < ROUNDS
        pair_data = jnp.concatenate([upper_block, lower_block], axis=1)
        rotation = rotation_of(summed_gram(pair_data, width))
        if not moving:
            rotated = jnp.dot(pair_data, rotation, preferred_element_type=jnp.float32)
            upper_block = rotated[:, :width].astype(jnp.bfloat16)
            lower_block = rotated[:, width:].astype(jnp.bfloat16)
            break
        first_columns = rotation[:, :width]
        second_columns = rotation[:, width:]
        going_right = jnp.dot(
            pair_data,
            jnp.where(position == 0, second_columns, first_columns),
            preferred_element_type=jnp.float32,
        ).astype(jnp.bfloat16)
        going_left = jnp.dot(
            pair_data,
            jnp.where(position == 0, first_columns, second_columns),
            preferred_element_type=jnp.float32,
        ).astype(jnp.bfloat16)
        from_left = send_right(going_right)
        from_right = send_left(going_left)
        upper_block = jnp.where(position == 0, going_left, from_left)
        lower_block = jnp.where(position == device_count - 1, going_right, from_right)
    gathered_design = jnp.concatenate([upper_block, lower_block], axis=1)
    squares = with_partner(jnp.sum(jnp.square(gathered_design.astype(jnp.float32)), axis=0))
    record_total = records * lax.axis_size(RECORD_AXES)
    column_rms = jnp.sqrt(squares / record_total + 1e-06)
    start = lax.axis_index(GROUP_AXES) * records
    rotated_design = lax.dynamic_slice_in_dim(gathered_design, start, records, axis=0)
    return (rotated_design, column_rms)


def solution(mesh):
    devices = mesh.devices.reshape(2, mesh.devices.shape[0] // 4, 2, 2, mesh.devices.shape[1] // 4, 2)
    view = Mesh(devices, COLUMN_AXES + RECORD_AXES)
    placed = (P(RECORD_AXES, COLUMN_AXES), P(RECORD_AXES))
    return jax.shard_map(
        local,
        mesh=view,
        in_specs=placed,
        out_specs=(P(RECORD_AXES, COLUMN_AXES), P(COLUMN_AXES)),
        check_vma=False,
    )
```

```python
import jax
import jax.numpy as jnp
from jax import lax
from jax.experimental import pallas as pl
from jax.experimental.pallas import tpu as pltpu
from jax.sharding import Mesh, PartitionSpec as P

ROUNDS = 3
SWEEPS = 6


eps_angle = 0.01


COLUMN_AXES = ("x_lo", "z", "core")
GROUP_AXES = ("x_hi", "y_hi")
PAIR_AXIS = "y_lo"
RECORD_AXES = GROUP_AXES + (PAIR_AXIS,)


def from_behind(value, steps):
    count = lax.axis_size(COLUMN_AXES)
    leading, last = (max(0, -steps), min(count, count - steps))
    return lax.ppermute(value, COLUMN_AXES, [(source, source + steps) for source in range(leading, last)])


PARTNER_AXES = ("core", "y_hi", PAIR_AXIS)


def partner_pairs(halves):
    pairs = []
    for half in range(halves):
        for core, other in ((0, half), (1, (half - 1) % halves)):
            even, odd = (core * halves + half) * 2, (core * halves + other) * 2 + 1
            pairs += [(even, odd), (odd, even)]
    return pairs


def from_partner(value):
    return lax.ppermute(value, PARTNER_AXES, partner_pairs(lax.axis_size("y_hi")))


def with_partner(value):
    return value + from_partner(value)


def diagonal_of(matrix):
    size = matrix.shape[0]
    rows = lax.broadcasted_iota(jnp.int32, (size, size), 0)
    cols = lax.broadcasted_iota(jnp.int32, (size, size), 1)
    return jnp.sum(jnp.where(rows == cols, matrix, 0.0), axis=0)


def half_angle_terms(first_diag, second_diag, coupling):
    spread = second_diag - first_diag
    tangent = (
        2.0
        * coupling
        * spread
        / (
            spread * spread
            + 4.0 * coupling * coupling
            + eps_angle * (first_diag + second_diag) ** 2
        )
    )
    double_cos = 1.0 / jnp.sqrt(1.0 + tangent * tangent)
    cosine = jnp.sqrt(0.5 + 0.5 * double_cos)
    sine_value = tangent * double_cos / (2.0 * cosine)
    return cosine, sine_value


def sweeps_kernel(local_ref, received_ref, rotation_ref):
    width = local_ref.shape[1]
    rows = lax.broadcasted_iota(jnp.int32, (width, width), 0)
    cols = lax.broadcasted_iota(jnp.int32, (width, width), 1)
    on_diagonal = rows == cols
    folded = local_ref[:width, :] + received_ref[:width, :]
    top_right = local_ref[width : 2 * width, :] + received_ref[width : 2 * width, :]
    low_diag = (local_ref[2 * width : 2 * width + 8, :] + received_ref[2 * width : 2 * width + 8, :])[:1, :]
    mirrored = folded.T
    top_left = jnp.where(rows <= cols, folded, mirrored)
    low_right = jnp.where(rows > cols, folded, jnp.where(rows < cols, mirrored, low_diag))
    low_left = top_right.T
    first_top = jnp.where(on_diagonal, 1.0, 0.0).astype(jnp.float32)
    first_low = jnp.zeros((width, width), jnp.float32)
    second_top = jnp.zeros((width, width), jnp.float32)
    second_low = first_top

    def diagonal_row(matrix):
        return jnp.sum(jnp.where(on_diagonal, matrix, 0.0), axis=0, keepdims=True)

    def as_column(row):
        return jnp.broadcast_to(row, (128, width)).T[:, :1]

    def to_left(matrix, axis):
        return pltpu.roll(matrix, width - 1, axis)

    for sweep_index in range(SWEEPS):
        if sweep_index > 0:
            top_right = to_left(top_right, 1)
            low_left = to_left(low_left, 0)
            low_right = to_left(to_left(low_right, 0), 1)
            second_top = to_left(second_top, 1)
            second_low = to_left(second_low, 1)
        cos_col, sin_col = half_angle_terms(
            diagonal_row(top_left), diagonal_row(low_right), diagonal_row(top_right)
        )
        cos_row = as_column(cos_col)
        sin_row = as_column(sin_col)
        left_a = top_left * cos_col - top_right * sin_col
        right_a = top_left * sin_col + top_right * cos_col
        left_b = low_left * cos_col - low_right * sin_col
        right_b = low_left * sin_col + low_right * cos_col
        top_left = cos_row * left_a - sin_row * left_b
        low_left = sin_row * left_a + cos_row * left_b
        top_right = cos_row * right_a - sin_row * right_b
        low_right = sin_row * right_a + cos_row * right_b
        first_top, second_top = (
            first_top * cos_col - second_top * sin_col,
            first_top * sin_col + second_top * cos_col,
        )
        first_low, second_low = (
            first_low * cos_col - second_low * sin_col,
            first_low * sin_col + second_low * cos_col,
        )
    second_top = pltpu.roll(second_top, SWEEPS - 1, 1)
    second_low = pltpu.roll(second_low, SWEEPS - 1, 1)
    out = rotation_ref.dtype
    rotation_ref[:width, :width] = first_top.astype(out)
    rotation_ref[width:, :width] = first_low.astype(out)
    rotation_ref[:width, width:] = second_top.astype(out)
    rotation_ref[width:, width:] = second_low.astype(out)


def rotation_of(local, received):
    width = local.shape[1]
    vmem = pl.BlockSpec(memory_space=pltpu.VMEM)
    return pl.pallas_call(
        sweeps_kernel,
        out_shape=jax.ShapeDtypeStruct((2 * width, 2 * width), jnp.bfloat16),
        in_specs=[vmem, vmem],
        out_specs=vmem,
        cost_estimate=pl.CostEstimate(
            flops=SWEEPS * 40 * width * width, transcendentals=SWEEPS * 8 * width, bytes_accessed=4 * 4 * width * width
        ),
    )(local, received)


def send_right(block):
    return from_behind(block, 1)


def send_left(block):
    return from_behind(block, -1)


def inner_products(left_part, right_part):
    return lax.dot_general(
        left_part, right_part, (((0,), (0,)), ((), ())), preferred_element_type=jnp.float32
    )


def gathered_records(block):
    count = lax.axis_size(GROUP_AXES)
    spread = jnp.broadcast_to(block[None], (count,) + block.shape)
    gathered = lax.all_to_all(spread, GROUP_AXES, 0, 0, tiled=False)
    return gathered.reshape(count * block.shape[0], block.shape[1])


def summed_gram(pair_data, width):
    gram_local = inner_products(pair_data, pair_data)
    top_left = gram_local[:width, :width]
    top_right = gram_local[:width, width:]
    low_right = gram_local[width:, width:]
    rows = lax.broadcasted_iota(jnp.int32, (width, width), 0)
    cols = lax.broadcasted_iota(jnp.int32, (width, width), 1)
    folded = jnp.where(rows <= cols, top_left, low_right)
    padded = -(-(2 * width + 1) // 8) * 8
    packed = jnp.concatenate(
        [
            folded,
            top_right,
            diagonal_of(low_right)[None, :],
            jnp.zeros((padded - 2 * width - 1, width), jnp.float32),
        ],
        axis=0,
    )
    return packed, from_partner(packed)


def local(design, record_weight):
    width = design.shape[1] // 2
    records = design.shape[0]
    weighted = (design.astype(jnp.float32) * record_weight[:, None]).astype(jnp.bfloat16)
    weighted = gathered_records(weighted)
    upper_block = weighted[:, :width]
    lower_block = weighted[:, width:]
    position = lax.axis_index(COLUMN_AXES)
    device_count = lax.axis_size(COLUMN_AXES)
    for round_index in range(ROUNDS):
        moving = round_index + 1 < ROUNDS
        pair_data = jnp.concatenate([upper_block, lower_block], axis=1)
        rotation = rotation_of(*summed_gram(pair_data, width))
        if not moving:
            rotated = jnp.dot(pair_data, rotation, preferred_element_type=jnp.float32)
            upper_block = rotated[:, :width].astype(jnp.bfloat16)
            lower_block = rotated[:, width:].astype(jnp.bfloat16)
            break
        first_columns = rotation[:, :width]
        second_columns = rotation[:, width:]
        going_right = jnp.dot(
            pair_data,
            jnp.where(position == 0, second_columns, first_columns),
            preferred_element_type=jnp.float32,
        ).astype(jnp.bfloat16)
        going_left = jnp.dot(
            pair_data,
            jnp.where(position == 0, first_columns, second_columns),
            preferred_element_type=jnp.float32,
        ).astype(jnp.bfloat16)
        from_left = send_right(going_right)
        from_right = send_left(going_left)
        upper_block = jnp.where(position == 0, going_left, from_left)
        lower_block = jnp.where(position == device_count - 1, going_right, from_right)
    gathered_design = jnp.concatenate([upper_block, lower_block], axis=1)
    squares = with_partner(jnp.sum(jnp.square(gathered_design.astype(jnp.float32)), axis=0))
    record_total = records * lax.axis_size(RECORD_AXES)
    column_rms = jnp.sqrt(squares / record_total + 1e-06)
    start = lax.axis_index(GROUP_AXES) * records
    rotated_design = lax.dynamic_slice_in_dim(gathered_design, start, records, axis=0)
    return (rotated_design, column_rms)


def solution(mesh):
    devices = mesh.devices.reshape(2, mesh.devices.shape[0] // 4, 2, 2, mesh.devices.shape[1] // 4, 2)
    view = Mesh(devices, COLUMN_AXES + RECORD_AXES)
    placed = (P(RECORD_AXES, COLUMN_AXES), P(RECORD_AXES))
    return jax.shard_map(
        local,
        mesh=view,
        in_specs=placed,
        out_specs=(P(RECORD_AXES, COLUMN_AXES), P(COLUMN_AXES)),
        check_vma=False,
    )
```

```python
import jax
import jax.numpy as jnp
from jax import lax
from jax.experimental import pallas as pl
from jax.experimental.pallas import tpu as pltpu
from jax.sharding import Mesh, PartitionSpec as P

ROUNDS = 3
SWEEPS = 6


eps_angle = 0.01


COLUMN_AXES = ("x_lo", "z", "core")
GROUP_AXES = ("x_hi", "y_hi")
PAIR_AXIS = "y_lo"
RECORD_AXES = GROUP_AXES + (PAIR_AXIS,)


def from_behind(value, steps):
    count = lax.axis_size(COLUMN_AXES)
    leading, last = (max(0, -steps), min(count, count - steps))
    return lax.ppermute(value, COLUMN_AXES, [(source, source + steps) for source in range(leading, last)])


PARTNER_AXES = ("core", "y_hi", PAIR_AXIS)


def partner_pairs(halves):
    pairs = []
    for half in range(halves):
        for core, other in ((0, half), (1, (half - 1) % halves)):
            even, odd = (core * halves + half) * 2, (core * halves + other) * 2 + 1
            pairs += [(even, odd), (odd, even)]
    return pairs


def from_partner(value):
    return lax.ppermute(value, PARTNER_AXES, partner_pairs(lax.axis_size("y_hi")))


def with_partner(value):
    return value + from_partner(value)


def diagonal_of(matrix):
    size = matrix.shape[0]
    rows = lax.broadcasted_iota(jnp.int32, (size, size), 0)
    cols = lax.broadcasted_iota(jnp.int32, (size, size), 1)
    return jnp.sum(jnp.where(rows == cols, matrix, 0.0), axis=0)


def half_angle_terms(first_diag, second_diag, coupling):
    spread = second_diag - first_diag
    tangent = (
        2.0
        * coupling
        * spread
        / (
            spread * spread
            + 4.0 * coupling * coupling
            + eps_angle * (first_diag + second_diag) ** 2
        )
    )
    double_cos = 1.0 / jnp.sqrt(1.0 + tangent * tangent)
    cosine = jnp.sqrt(0.5 + 0.5 * double_cos)
    sine_value = tangent * double_cos / (2.0 * cosine)
    return cosine, sine_value


def sweeps_kernel(local_ref, received_ref, rotation_ref):
    width = local_ref.shape[1]
    rows = lax.broadcasted_iota(jnp.int32, (width, width), 0)
    cols = lax.broadcasted_iota(jnp.int32, (width, width), 1)
    on_diagonal = rows == cols
    folded = local_ref[:width, :] + received_ref[:width, :]
    top_right = local_ref[width : 2 * width, :] + received_ref[width : 2 * width, :]
    low_diag = (local_ref[2 * width : 2 * width + 8, :] + received_ref[2 * width : 2 * width + 8, :])[:1, :]
    mirrored = folded.T
    top_left = jnp.where(rows <= cols, folded, mirrored)
    low_right = jnp.where(rows > cols, folded, jnp.where(rows < cols, mirrored, low_diag))
    low_left = top_right.T
    first_top = jnp.where(on_diagonal, 1.0, 0.0).astype(jnp.float32)
    first_low = jnp.zeros((width, width), jnp.float32)
    second_top = jnp.zeros((width, width), jnp.float32)
    second_low = first_top

    def diagonal_row(matrix):
        return jnp.sum(jnp.where(on_diagonal, matrix, 0.0), axis=0, keepdims=True)

    def as_column(row):
        return jnp.broadcast_to(row, (128, width)).T[:, :1]

    def to_left(matrix, axis):
        return pltpu.roll(matrix, width - 1, axis)

    for sweep_index in range(SWEEPS):
        if sweep_index > 0:
            top_right = to_left(top_right, 1)
            low_left = to_left(low_left, 0)
            low_right = to_left(to_left(low_right, 0), 1)
            second_top = to_left(second_top, 1)
            second_low = to_left(second_low, 1)
        cos_col, sin_col = half_angle_terms(
            diagonal_row(top_left), diagonal_row(low_right), diagonal_row(top_right)
        )
        cos_row = as_column(cos_col)
        sin_row = as_column(sin_col)
        left_a = top_left * cos_col - top_right * sin_col
        right_a = top_left * sin_col + top_right * cos_col
        left_b = low_left * cos_col - low_right * sin_col
        right_b = low_left * sin_col + low_right * cos_col
        top_left = cos_row * left_a - sin_row * left_b
        low_left = sin_row * left_a + cos_row * left_b
        top_right = cos_row * right_a - sin_row * right_b
        low_right = sin_row * right_a + cos_row * right_b
        first_top, second_top = (
            first_top * cos_col - second_top * sin_col,
            first_top * sin_col + second_top * cos_col,
        )
        first_low, second_low = (
            first_low * cos_col - second_low * sin_col,
            first_low * sin_col + second_low * cos_col,
        )
    second_top = pltpu.roll(second_top, SWEEPS - 1, 1)
    second_low = pltpu.roll(second_low, SWEEPS - 1, 1)
    out = rotation_ref.dtype
    rotation_ref[:width, :width] = first_top.astype(out)
    rotation_ref[width:, :width] = first_low.astype(out)
    rotation_ref[:width, width:] = second_top.astype(out)
    rotation_ref[width:, width:] = second_low.astype(out)


def rotation_of(local, received):
    width = local.shape[1]
    vmem = pl.BlockSpec(memory_space=pltpu.VMEM)
    return pl.pallas_call(
        sweeps_kernel,
        out_shape=jax.ShapeDtypeStruct((2 * width, 2 * width), jnp.bfloat16),
        in_specs=[vmem, vmem],
        out_specs=vmem,
        cost_estimate=pl.CostEstimate(
            flops=SWEEPS * 40 * width * width, transcendentals=SWEEPS * 8 * width, bytes_accessed=4 * 4 * width * width
        ),
    )(local, received)


def send_right(block):
    return from_behind(block, 1)


def send_left(block):
    return from_behind(block, -1)


def inner_products(left_part, right_part):
    return lax.dot_general(
        left_part, right_part, (((0,), (0,)), ((), ())), preferred_element_type=jnp.float32
    )


def gathered_records(block):
    count = lax.axis_size(GROUP_AXES)
    spread = jnp.broadcast_to(block[None], (count,) + block.shape)
    gathered = lax.all_to_all(spread, GROUP_AXES, 0, 0, tiled=False)
    return gathered.reshape(count * block.shape[0], block.shape[1])


def summed_gram(pair_data, width):
    gram_local = inner_products(pair_data, pair_data)
    top_left = gram_local[:width, :width]
    top_right = gram_local[:width, width:]
    low_right = gram_local[width:, width:]
    rows = lax.broadcasted_iota(jnp.int32, (width, width), 0)
    cols = lax.broadcasted_iota(jnp.int32, (width, width), 1)
    folded = jnp.where(rows <= cols, top_left, low_right)
    padded = -(-(2 * width + 1) // 8) * 8
    packed = jnp.concatenate(
        [
            folded,
            top_right,
            diagonal_of(low_right)[None, :],
            jnp.zeros((padded - 2 * width - 1, width), jnp.float32),
        ],
        axis=0,
    )
    return packed, from_partner(packed)


def local(design, record_weight):
    width = design.shape[1] // 2
    records = design.shape[0]
    count = lax.axis_size(GROUP_AXES)
    spread = (
        jnp.broadcast_to(design[None], (count,) + design.shape).astype(jnp.float32)
        * record_weight[None, :, None]
    ).astype(jnp.bfloat16)
    weighted = lax.all_to_all(spread, GROUP_AXES, 0, 0, tiled=False).reshape(
        count * records, design.shape[1]
    )
    upper_block = weighted[:, :width]
    lower_block = weighted[:, width:]
    position = lax.axis_index(COLUMN_AXES)
    device_count = lax.axis_size(COLUMN_AXES)
    for round_index in range(ROUNDS):
        moving = round_index + 1 < ROUNDS
        pair_data = jnp.concatenate([upper_block, lower_block], axis=1)
        rotation = rotation_of(*summed_gram(pair_data, width))
        if not moving:
            break
        first_columns = rotation[:, :width]
        second_columns = rotation[:, width:]
        going_right = jnp.dot(
            pair_data,
            jnp.where(position == 0, second_columns, first_columns),
            preferred_element_type=jnp.float32,
        ).astype(jnp.bfloat16)
        going_left = jnp.dot(
            pair_data,
            jnp.where(position == 0, first_columns, second_columns),
            preferred_element_type=jnp.float32,
        ).astype(jnp.bfloat16)
        from_left = send_right(going_right)
        from_right = send_left(going_left)
        upper_block = jnp.where(position == 0, going_left, from_left)
        lower_block = jnp.where(position == device_count - 1, going_right, from_right)
    rotated = jnp.dot(pair_data, rotation, preferred_element_type=jnp.float32).astype(jnp.bfloat16)
    squares = with_partner(jnp.sum(jnp.square(rotated.astype(jnp.float32)), axis=0))
    record_total = records * lax.axis_size(RECORD_AXES)
    column_rms = jnp.sqrt(squares / record_total + 1e-06)
    start = lax.axis_index(GROUP_AXES) * records
    own_rows = lax.dynamic_slice_in_dim(pair_data, start, records, axis=0)
    rotated_design = jnp.dot(own_rows, rotation, preferred_element_type=jnp.float32).astype(jnp.bfloat16)
    return (rotated_design, column_rms)


def solution(mesh):
    devices = mesh.devices.reshape(2, mesh.devices.shape[0] // 4, 2, 2, mesh.devices.shape[1] // 4, 2)
    view = Mesh(devices, COLUMN_AXES + RECORD_AXES)
    placed = (P(RECORD_AXES, COLUMN_AXES), P(RECORD_AXES))
    return jax.shard_map(
        local,
        mesh=view,
        in_specs=placed,
        out_specs=(P(RECORD_AXES, COLUMN_AXES), P(COLUMN_AXES)),
        check_vma=False,
    )
```

```python
import jax
import jax.numpy as jnp
from jax import lax
from jax.experimental import pallas as pl
from jax.experimental.pallas import tpu as pltpu
from jax.sharding import Mesh, PartitionSpec as P

ROUNDS = 3
SWEEPS = 6


eps_angle = 0.01


COLUMN_AXES = ("x_lo", "z", "core")
GROUP_AXES = ("x_hi", "y_hi")
PAIR_AXIS = "y_lo"
RECORD_AXES = GROUP_AXES + (PAIR_AXIS,)


def from_behind(value, steps):
    count = lax.axis_size(COLUMN_AXES)
    leading, last = (max(0, -steps), min(count, count - steps))
    return lax.ppermute(value, COLUMN_AXES, [(source, source + steps) for source in range(leading, last)])


PARTNER_AXES = ("core", "y_hi", PAIR_AXIS)


def partner_pairs(halves):
    pairs = []
    for half in range(halves):
        for core, other in ((0, half), (1, (half - 1) % halves)):
            even, odd = (core * halves + half) * 2, (core * halves + other) * 2 + 1
            pairs += [(even, odd), (odd, even)]
    return pairs


def from_partner(value):
    return lax.ppermute(value, PARTNER_AXES, partner_pairs(lax.axis_size("y_hi")))


def with_partner(value):
    return value + from_partner(value)


def diagonal_of(matrix):
    size = matrix.shape[0]
    rows = lax.broadcasted_iota(jnp.int32, (size, size), 0)
    cols = lax.broadcasted_iota(jnp.int32, (size, size), 1)
    return jnp.sum(jnp.where(rows == cols, matrix, 0.0), axis=0)


def half_angle_terms(first_diag, second_diag, coupling):
    spread = second_diag - first_diag
    tangent = (
        2.0
        * coupling
        * spread
        / (
            spread * spread
            + 4.0 * coupling * coupling
            + eps_angle * (first_diag + second_diag) ** 2
        )
    )
    double_cos = 1.0 / jnp.sqrt(1.0 + tangent * tangent)
    cosine = jnp.sqrt(0.5 + 0.5 * double_cos)
    sine_value = tangent * double_cos / (2.0 * cosine)
    return cosine, sine_value


def sweeps_kernel(local_ref, received_hbm, rotation_ref, received_ref, copy_sem):
    width = local_ref.shape[1]
    arrival = pltpu.make_async_copy(received_hbm, received_ref, copy_sem)
    arrival.start()
    rows = lax.broadcasted_iota(jnp.int32, (width, width), 0)
    cols = lax.broadcasted_iota(jnp.int32, (width, width), 1)
    on_diagonal = rows == cols
    arrival.wait()
    folded = local_ref[:width, :] + received_ref[:width, :]
    top_right = local_ref[width : 2 * width, :] + received_ref[width : 2 * width, :]
    low_diag = (local_ref[2 * width : 2 * width + 8, :] + received_ref[2 * width : 2 * width + 8, :])[:1, :]
    mirrored = folded.T
    top_left = jnp.where(rows <= cols, folded, mirrored)
    low_right = jnp.where(rows > cols, folded, jnp.where(rows < cols, mirrored, low_diag))
    first_top = jnp.where(on_diagonal, 1.0, 0.0).astype(jnp.float32)
    first_low = jnp.zeros((width, width), jnp.float32)
    second_top = jnp.zeros((width, width), jnp.float32)
    second_low = first_top

    def diagonal_row(matrix):
        return jnp.sum(jnp.where(on_diagonal, matrix, 0.0), axis=0, keepdims=True)

    def as_column(row):
        return jnp.broadcast_to(row, (128, width)).T[:, :1]

    def to_left(matrix, axis):
        return pltpu.roll(matrix, width - 1, axis)

    for sweep_index in range(SWEEPS):
        if sweep_index > 0:
            top_right = to_left(top_right, 1)
            low_right = to_left(to_left(low_right, 0), 1)
            second_top = to_left(second_top, 1)
            second_low = to_left(second_low, 1)
        low_left = top_right.T
        cos_col, sin_col = half_angle_terms(
            diagonal_row(top_left), diagonal_row(low_right), diagonal_row(top_right)
        )
        cos_row = as_column(cos_col)
        sin_row = as_column(sin_col)
        left_a = top_left * cos_col - top_right * sin_col
        right_a = top_left * sin_col + top_right * cos_col
        left_b = low_left * cos_col - low_right * sin_col
        right_b = low_left * sin_col + low_right * cos_col
        top_left = cos_row * left_a - sin_row * left_b
        top_right = cos_row * right_a - sin_row * right_b
        low_right = sin_row * right_a + cos_row * right_b
        first_top, second_top = (
            first_top * cos_col - second_top * sin_col,
            first_top * sin_col + second_top * cos_col,
        )
        first_low, second_low = (
            first_low * cos_col - second_low * sin_col,
            first_low * sin_col + second_low * cos_col,
        )
    second_top = pltpu.roll(second_top, SWEEPS - 1, 1)
    second_low = pltpu.roll(second_low, SWEEPS - 1, 1)
    out = rotation_ref.dtype
    rotation_ref[:width, :width] = first_top.astype(out)
    rotation_ref[width:, :width] = first_low.astype(out)
    rotation_ref[:width, width:] = second_top.astype(out)
    rotation_ref[width:, width:] = second_low.astype(out)


def rotation_of(local, received):
    width = local.shape[1]
    vmem = pl.BlockSpec(memory_space=pltpu.VMEM)
    return pl.pallas_call(
        sweeps_kernel,
        out_shape=jax.ShapeDtypeStruct((2 * width, 2 * width), jnp.bfloat16),
        in_specs=[vmem, pl.BlockSpec(memory_space=pl.ANY)],
        out_specs=vmem,
        scratch_shapes=[pltpu.VMEM(received.shape, received.dtype), pltpu.SemaphoreType.DMA(())],
        cost_estimate=pl.CostEstimate(
            flops=SWEEPS * 40 * width * width, transcendentals=SWEEPS * 8 * width, bytes_accessed=4 * 4 * width * width
        ),
    )(local, received)


def send_right(block):
    return from_behind(block, 1)


def send_left(block):
    return from_behind(block, -1)


def inner_products(left_part, right_part):
    return lax.dot_general(
        left_part, right_part, (((0,), (0,)), ((), ())), preferred_element_type=jnp.float32
    )


def gathered_records(block):
    count = lax.axis_size(GROUP_AXES)
    spread = jnp.broadcast_to(block[None], (count,) + block.shape)
    gathered = lax.all_to_all(spread, GROUP_AXES, 0, 0, tiled=False)
    return gathered.reshape(count * block.shape[0], block.shape[1])


def summed_gram(pair_data, width):
    gram_local = inner_products(pair_data, pair_data)
    top_left = gram_local[:width, :width]
    top_right = gram_local[:width, width:]
    low_right = gram_local[width:, width:]
    rows = lax.broadcasted_iota(jnp.int32, (width, width), 0)
    cols = lax.broadcasted_iota(jnp.int32, (width, width), 1)
    folded = jnp.where(rows <= cols, top_left, low_right)
    padded = -(-(2 * width + 1) // 8) * 8
    packed = jnp.concatenate(
        [
            folded,
            top_right,
            diagonal_of(low_right)[None, :],
            jnp.zeros((padded - 2 * width - 1, width), jnp.float32),
        ],
        axis=0,
    )
    return packed, from_partner(packed)


def local(design, record_weight):
    width = design.shape[1] // 2
    records = design.shape[0]
    weighted = (design.astype(jnp.float32) * record_weight[:, None]).astype(jnp.bfloat16)
    weighted = gathered_records(weighted)
    upper_block = weighted[:, :width]
    lower_block = weighted[:, width:]
    position = lax.axis_index(COLUMN_AXES)
    device_count = lax.axis_size(COLUMN_AXES)
    for round_index in range(ROUNDS):
        moving = round_index + 1 < ROUNDS
        pair_data = jnp.concatenate([upper_block, lower_block], axis=1)
        rotation = rotation_of(*summed_gram(pair_data, width))
        if not moving:
            rotated = jnp.dot(pair_data, rotation, preferred_element_type=jnp.float32)
            upper_block = rotated[:, :width].astype(jnp.bfloat16)
            lower_block = rotated[:, width:].astype(jnp.bfloat16)
            break
        first_columns = rotation[:, :width]
        second_columns = rotation[:, width:]
        going_right = jnp.dot(
            pair_data,
            jnp.where(position == 0, second_columns, first_columns),
            preferred_element_type=jnp.float32,
        ).astype(jnp.bfloat16)
        going_left = jnp.dot(
            pair_data,
            jnp.where(position == 0, first_columns, second_columns),
            preferred_element_type=jnp.float32,
        ).astype(jnp.bfloat16)
        from_left = send_right(going_right)
        from_right = send_left(going_left)
        upper_block = jnp.where(position == 0, going_left, from_left)
        lower_block = jnp.where(position == device_count - 1, going_right, from_right)
    gathered_design = jnp.concatenate([upper_block, lower_block], axis=1)
    squares = with_partner(jnp.sum(jnp.square(gathered_design.astype(jnp.float32)), axis=0))
    record_total = records * lax.axis_size(RECORD_AXES)
    column_rms = jnp.sqrt(squares / record_total + 1e-06)
    start = lax.axis_index(GROUP_AXES) * records
    rotated_design = lax.dynamic_slice_in_dim(gathered_design, start, records, axis=0)
    return (rotated_design, column_rms)


def solution(mesh):
    devices = mesh.devices.reshape(2, mesh.devices.shape[0] // 4, 2, 2, mesh.devices.shape[1] // 4, 2)
    view = Mesh(devices, COLUMN_AXES + RECORD_AXES)
    placed = (P(RECORD_AXES, COLUMN_AXES), P(RECORD_AXES))
    return jax.shard_map(
        local,
        mesh=view,
        in_specs=placed,
        out_specs=(P(RECORD_AXES, COLUMN_AXES), P(COLUMN_AXES)),
        check_vma=False,
    )
```

```python
import jax
import jax.numpy as jnp
from jax import lax
from jax.experimental import pallas as pl
from jax.experimental.pallas import tpu as pltpu
from jax.sharding import Mesh, PartitionSpec as P

ROUNDS = 3
SWEEPS = 6


eps_angle = 0.01


COLUMN_AXES = ("x_lo", "z", "core")
GROUP_AXES = ("x_hi", "y_hi")
PAIR_AXIS = "y_lo"
RECORD_AXES = GROUP_AXES + (PAIR_AXIS,)


def from_behind(value, steps):
    count = lax.axis_size(COLUMN_AXES)
    leading, last = (max(0, -steps), min(count, count - steps))
    return lax.ppermute(value, COLUMN_AXES, [(source, source + steps) for source in range(leading, last)])


PARTNER_AXES = ("core", "y_hi", PAIR_AXIS)


def partner_pairs(halves):
    pairs = []
    for half in range(halves):
        for core, other in ((0, half), (1, (half - 1) % halves)):
            even, odd = (core * halves + half) * 2, (core * halves + other) * 2 + 1
            pairs += [(even, odd), (odd, even)]
    return pairs


def from_partner(value):
    return lax.ppermute(value, PARTNER_AXES, partner_pairs(lax.axis_size("y_hi")))


def with_partner(value):
    return value + from_partner(value)


def diagonal_of(matrix):
    size = matrix.shape[0]
    rows = lax.broadcasted_iota(jnp.int32, (size, size), 0)
    cols = lax.broadcasted_iota(jnp.int32, (size, size), 1)
    return jnp.sum(jnp.where(rows == cols, matrix, 0.0), axis=0)


def half_angle_terms(first_diag, second_diag, coupling):
    spread = second_diag - first_diag
    tangent = (
        2.0
        * coupling
        * spread
        / (
            spread * spread
            + 4.0 * coupling * coupling
            + eps_angle * (first_diag + second_diag) ** 2
        )
    )
    double_cos = 1.0 / jnp.sqrt(1.0 + tangent * tangent)
    cosine = jnp.sqrt(0.5 + 0.5 * double_cos)
    sine_value = tangent * double_cos / (2.0 * cosine)
    return cosine, sine_value


def sweeps_kernel(local_ref, received_ref, rotation_ref):
    width = local_ref.shape[1]
    rows = lax.broadcasted_iota(jnp.int32, (width, width), 0)
    cols = lax.broadcasted_iota(jnp.int32, (width, width), 1)
    on_diagonal = rows == cols
    folded = local_ref[:width, :] + received_ref[:width, :]
    top_right = local_ref[width : 2 * width, :] + received_ref[width : 2 * width, :]
    low_diag = (local_ref[2 * width : 2 * width + 8, :] + received_ref[2 * width : 2 * width + 8, :])[:1, :]
    mirrored = folded.T
    top_left = jnp.where(rows <= cols, folded, mirrored)
    low_right = jnp.where(rows > cols, folded, jnp.where(rows < cols, mirrored, low_diag))
    low_left = top_right.T
    first_top = jnp.where(on_diagonal, 1.0, 0.0).astype(jnp.float32)
    first_low = jnp.zeros((width, width), jnp.float32)
    second_top = jnp.zeros((width, width), jnp.float32)
    second_low = first_top

    def diagonal_row(matrix):
        return jnp.sum(jnp.where(on_diagonal, matrix, 0.0), axis=0, keepdims=True)

    def as_column(row):
        return jnp.broadcast_to(row, (128, width)).T[:, :1]

    def to_left(matrix, axis):
        return pltpu.roll(matrix, width - 1, axis)

    for sweep_index in range(SWEEPS):
        if sweep_index > 0:
            top_right = to_left(top_right, 1)
            low_left = to_left(low_left, 0)
            low_right = to_left(to_left(low_right, 0), 1)
            second_top = to_left(second_top, 1)
            second_low = to_left(second_low, 1)
        cos_col, sin_col = half_angle_terms(
            diagonal_row(top_left), diagonal_row(low_right), diagonal_row(top_right)
        )
        cos_row = as_column(cos_col)
        sin_row = as_column(sin_col)
        left_a = top_left * cos_col - top_right * sin_col
        right_a = top_left * sin_col + top_right * cos_col
        left_b = low_left * cos_col - low_right * sin_col
        right_b = low_left * sin_col + low_right * cos_col
        top_left = cos_row * left_a - sin_row * left_b
        low_left = sin_row * left_a + cos_row * left_b
        top_right = cos_row * right_a - sin_row * right_b
        low_right = sin_row * right_a + cos_row * right_b
        first_top, second_top = (
            first_top * cos_col - second_top * sin_col,
            first_top * sin_col + second_top * cos_col,
        )
        first_low, second_low = (
            first_low * cos_col - second_low * sin_col,
            first_low * sin_col + second_low * cos_col,
        )
    second_top = pltpu.roll(second_top, SWEEPS - 1, 1)
    second_low = pltpu.roll(second_low, SWEEPS - 1, 1)
    out = rotation_ref.dtype
    rotation_ref[:width, :width] = first_top.astype(out)
    rotation_ref[width:, :width] = first_low.astype(out)
    rotation_ref[:width, width:] = second_top.astype(out)
    rotation_ref[width:, width:] = second_low.astype(out)


def rotation_of(local, received):
    width = local.shape[1]
    vmem = pl.BlockSpec(memory_space=pltpu.VMEM)
    return pl.pallas_call(
        sweeps_kernel,
        out_shape=jax.ShapeDtypeStruct((2 * width, 2 * width), jnp.bfloat16),
        in_specs=[vmem, vmem],
        out_specs=vmem,
        cost_estimate=pl.CostEstimate(
            flops=SWEEPS * 40 * width * width, transcendentals=SWEEPS * 8 * width, bytes_accessed=4 * 4 * width * width
        ),
    )(local, received)


def send_right(block):
    return from_behind(block, 1)


def send_left(block):
    return from_behind(block, -1)


def inner_products(left_part, right_part):
    return lax.dot_general(
        left_part, right_part, (((0,), (0,)), ((), ())), preferred_element_type=jnp.float32
    )


def gathered_records(block):
    count = lax.axis_size(GROUP_AXES)
    spread = jnp.broadcast_to(block[None], (count,) + block.shape)
    gathered = lax.all_to_all(spread, GROUP_AXES, 0, 0, tiled=False)
    return gathered.reshape(count * block.shape[0], block.shape[1])


def summed_gram(pair_data, width):
    gram_local = inner_products(pair_data, pair_data)
    top_left = gram_local[:width, :width]
    top_right = gram_local[:width, width:]
    low_right = gram_local[width:, width:]
    rows = lax.broadcasted_iota(jnp.int32, (width, width), 0)
    cols = lax.broadcasted_iota(jnp.int32, (width, width), 1)
    folded = jnp.where(rows <= cols, top_left, low_right)
    padded = -(-(2 * width + 1) // 8) * 8
    packed = jnp.concatenate(
        [
            folded,
            top_right,
            diagonal_of(low_right)[None, :],
            jnp.zeros((padded - 2 * width - 1, width), jnp.float32),
        ],
        axis=0,
    )
    return packed, from_partner(packed)


def local(design, record_weight):
    width = design.shape[1] // 2
    records = design.shape[0]
    weighted = (design.astype(jnp.float32) * record_weight[:, None]).astype(jnp.bfloat16)
    weighted = gathered_records(weighted)
    upper_block = weighted[:, :width]
    lower_block = weighted[:, width:]
    position = lax.axis_index(COLUMN_AXES)
    device_count = lax.axis_size(COLUMN_AXES)
    for round_index in range(ROUNDS):
        moving = round_index + 1 < ROUNDS
        pair_data = jnp.concatenate([upper_block, lower_block], axis=1)
        rotation = rotation_of(*summed_gram(pair_data, width))
        if not moving:
            break
        first_columns = rotation[:, :width]
        second_columns = rotation[:, width:]
        going_right = jnp.dot(
            pair_data,
            jnp.where(position == 0, second_columns, first_columns),
            preferred_element_type=jnp.float32,
        ).astype(jnp.bfloat16)
        going_left = jnp.dot(
            pair_data,
            jnp.where(position == 0, first_columns, second_columns),
            preferred_element_type=jnp.float32,
        ).astype(jnp.bfloat16)
        from_left = send_right(going_right)
        from_right = send_left(going_left)
        upper_block = jnp.where(position == 0, going_left, from_left)
        lower_block = jnp.where(position == device_count - 1, going_right, from_right)
    rotated = jnp.dot(pair_data, rotation, preferred_element_type=jnp.float32).astype(jnp.bfloat16)
    squares = with_partner(jnp.sum(jnp.square(rotated.astype(jnp.float32)), axis=0))
    record_total = records * lax.axis_size(RECORD_AXES)
    column_rms = jnp.sqrt(squares / record_total + 1e-06)
    start = lax.axis_index(GROUP_AXES) * records
    own_rows = lax.dynamic_slice_in_dim(pair_data, start, records, axis=0)
    rotated_design = jnp.dot(own_rows, rotation, preferred_element_type=jnp.float32).astype(jnp.bfloat16)
    return (rotated_design, column_rms)


def solution(mesh):
    devices = mesh.devices.reshape(2, mesh.devices.shape[0] // 4, 2, 2, mesh.devices.shape[1] // 4, 2)
    view = Mesh(devices, COLUMN_AXES + RECORD_AXES)
    placed = (P(RECORD_AXES, COLUMN_AXES), P(RECORD_AXES))
    return jax.shard_map(
        local,
        mesh=view,
        in_specs=placed,
        out_specs=(P(RECORD_AXES, COLUMN_AXES), P(COLUMN_AXES)),
        check_vma=False,
    )
```

```python
import jax
import jax.numpy as jnp
from jax import lax
from jax.experimental import pallas as pl
from jax.experimental.pallas import tpu as pltpu
from jax.sharding import Mesh, PartitionSpec as P

ROUNDS = 3
SWEEPS = 6


eps_angle = 0.01


COLUMN_AXES = ("x_lo", "z", "core")
GROUP_AXES = ("x_hi", "y_hi")
PAIR_AXIS = "y_lo"
RECORD_AXES = GROUP_AXES + (PAIR_AXIS,)


def from_behind(value, steps):
    count = lax.axis_size(COLUMN_AXES)
    leading, last = (max(0, -steps), min(count, count - steps))
    return lax.ppermute(value, COLUMN_AXES, [(source, source + steps) for source in range(leading, last)])


PARTNER_AXES = ("core", "y_hi", PAIR_AXIS)


def partner_pairs(halves):
    pairs = []
    for half in range(halves):
        for core, other in ((0, half), (1, (half - 1) % halves)):
            even, odd = (core * halves + half) * 2, (core * halves + other) * 2 + 1
            pairs += [(even, odd), (odd, even)]
    return pairs


def from_partner(value):
    return lax.ppermute(value, PARTNER_AXES, partner_pairs(lax.axis_size("y_hi")))


def with_partner(value):
    return value + from_partner(value)


def diagonal_of(matrix):
    size = matrix.shape[0]
    rows = lax.broadcasted_iota(jnp.int32, (size, size), 0)
    cols = lax.broadcasted_iota(jnp.int32, (size, size), 1)
    return jnp.sum(jnp.where(rows == cols, matrix, 0.0), axis=0)


def half_angle_terms(first_diag, second_diag, coupling):
    spread = second_diag - first_diag
    tangent = (
        2.0
        * coupling
        * spread
        / (
            spread * spread
            + 4.0 * coupling * coupling
            + eps_angle * (first_diag + second_diag) ** 2
        )
    )
    double_cos = 1.0 / jnp.sqrt(1.0 + tangent * tangent)
    cosine = jnp.sqrt(0.5 + 0.5 * double_cos)
    sine_value = tangent * double_cos / (2.0 * cosine)
    return cosine, sine_value


def sweeps_kernel(local_ref, received_ref, rotation_ref):
    width = local_ref.shape[1]
    rows = lax.broadcasted_iota(jnp.int32, (width, width), 0)
    cols = lax.broadcasted_iota(jnp.int32, (width, width), 1)
    on_diagonal = rows == cols
    folded = local_ref[:width, :] + received_ref[:width, :]
    top_right = local_ref[width : 2 * width, :] + received_ref[width : 2 * width, :]
    low_diag = (local_ref[2 * width : 2 * width + 8, :] + received_ref[2 * width : 2 * width + 8, :])[:1, :]
    mirrored = folded.T
    top_left = jnp.where(rows <= cols, folded, mirrored)
    low_right = jnp.where(rows > cols, folded, jnp.where(rows < cols, mirrored, low_diag))
    low_left = top_right.T
    first_top = jnp.where(on_diagonal, 1.0, 0.0).astype(jnp.float32)
    first_low = jnp.zeros((width, width), jnp.float32)
    second_top = jnp.zeros((width, width), jnp.float32)
    second_low = first_top

    def diagonal_row(matrix):
        return jnp.sum(jnp.where(on_diagonal, matrix, 0.0), axis=0, keepdims=True)

    def as_column(row):
        return jnp.broadcast_to(row, (128, width)).T[:, :1]

    def to_left(matrix, axis):
        return pltpu.roll(matrix, width - 1, axis)

    for sweep_index in range(SWEEPS):
        if sweep_index > 0:
            top_right = to_left(top_right, 1)
            low_left = to_left(low_left, 0)
            low_right = to_left(to_left(low_right, 0), 1)
            second_top = to_left(second_top, 1)
            second_low = to_left(second_low, 1)
        cos_col, sin_col = half_angle_terms(
            diagonal_row(top_left), diagonal_row(low_right), diagonal_row(top_right)
        )
        cos_row = as_column(cos_col)
        sin_row = as_column(sin_col)
        left_a = top_left * cos_col - top_right * sin_col
        right_a = top_left * sin_col + top_right * cos_col
        left_b = low_left * cos_col - low_right * sin_col
        right_b = low_left * sin_col + low_right * cos_col
        top_left = cos_row * left_a - sin_row * left_b
        low_left = sin_row * left_a + cos_row * left_b
        top_right = cos_row * right_a - sin_row * right_b
        low_right = sin_row * right_a + cos_row * right_b
        first_top, second_top = (
            first_top * cos_col - second_top * sin_col,
            first_top * sin_col + second_top * cos_col,
        )
        first_low, second_low = (
            first_low * cos_col - second_low * sin_col,
            first_low * sin_col + second_low * cos_col,
        )
    second_top = pltpu.roll(second_top, SWEEPS - 1, 1)
    second_low = pltpu.roll(second_low, SWEEPS - 1, 1)
    out = rotation_ref.dtype
    rotation_ref[:width, :width] = first_top.astype(out)
    rotation_ref[width:, :width] = first_low.astype(out)
    rotation_ref[:width, width:] = second_top.astype(out)
    rotation_ref[width:, width:] = second_low.astype(out)


def rotation_of(local, received):
    width = local.shape[1]
    vmem = pl.BlockSpec(memory_space=pltpu.VMEM)
    return pl.pallas_call(
        sweeps_kernel,
        out_shape=jax.ShapeDtypeStruct((2 * width, 2 * width), jnp.bfloat16),
        in_specs=[vmem, vmem],
        out_specs=vmem,
        cost_estimate=pl.CostEstimate(
            flops=SWEEPS * 40 * width * width, transcendentals=SWEEPS * 8 * width, bytes_accessed=4 * 4 * width * width
        ),
    )(local, received)


def send_right(block):
    return from_behind(block, 1)


def send_left(block):
    return from_behind(block, -1)


def inner_products(left_part, right_part):
    return lax.dot_general(
        left_part, right_part, (((0,), (0,)), ((), ())), preferred_element_type=jnp.float32
    )


def gathered_records(block):
    count = lax.axis_size(GROUP_AXES)
    spread = jnp.broadcast_to(block[None], (count,) + block.shape)
    gathered = lax.all_to_all(spread, GROUP_AXES, 0, 0, tiled=False)
    return gathered.reshape(count * block.shape[0], block.shape[1])


def summed_gram(pair_data, width):
    gram_local = inner_products(pair_data, pair_data)
    top_left = gram_local[:width, :width]
    top_right = gram_local[:width, width:]
    low_right = gram_local[width:, width:]
    rows = lax.broadcasted_iota(jnp.int32, (width, width), 0)
    cols = lax.broadcasted_iota(jnp.int32, (width, width), 1)
    folded = jnp.where(rows <= cols, top_left, low_right)
    padded = -(-(2 * width + 1) // 8) * 8
    packed = jnp.concatenate(
        [
            folded,
            top_right,
            diagonal_of(low_right)[None, :],
            jnp.zeros((padded - 2 * width - 1, width), jnp.float32),
        ],
        axis=0,
    )
    return packed, from_partner(packed)


def local(design, record_weight):
    width = design.shape[1] // 2
    records = design.shape[0]
    weighted = (design.astype(jnp.float32) * record_weight[:, None]).astype(jnp.bfloat16)
    weighted = gathered_records(weighted)
    upper_block = weighted[:, :width]
    lower_block = weighted[:, width:]
    position = lax.axis_index(COLUMN_AXES)
    device_count = lax.axis_size(COLUMN_AXES)
    for round_index in range(ROUNDS):
        moving = round_index + 1 < ROUNDS
        pair_data = jnp.concatenate([upper_block, lower_block], axis=1)
        rotation = rotation_of(*summed_gram(pair_data, width))
        if not moving:
            rotated = jnp.dot(pair_data, rotation, preferred_element_type=jnp.float32)
            upper_block = rotated[:, :width].astype(jnp.bfloat16)
            lower_block = rotated[:, width:].astype(jnp.bfloat16)
            break
        first_columns = rotation[:, :width]
        second_columns = rotation[:, width:]
        chosen = jnp.concatenate(
            [
                jnp.where(position == 0, second_columns, first_columns),
                jnp.where(position == 0, first_columns, second_columns),
            ],
            axis=1,
        )
        moving_blocks = jnp.dot(pair_data, chosen, preferred_element_type=jnp.float32).astype(
            jnp.bfloat16
        )
        going_right = moving_blocks[:, :width]
        going_left = moving_blocks[:, width:]
        from_left = send_right(going_right)
        from_right = send_left(going_left)
        upper_block = jnp.where(position == 0, going_left, from_left)
        lower_block = jnp.where(position == device_count - 1, going_right, from_right)
    gathered_design = jnp.concatenate([upper_block, lower_block], axis=1)
    squares = with_partner(jnp.sum(jnp.square(gathered_design.astype(jnp.float32)), axis=0))
    record_total = records * lax.axis_size(RECORD_AXES)
    column_rms = jnp.sqrt(squares / record_total + 1e-06)
    start = lax.axis_index(GROUP_AXES) * records
    rotated_design = lax.dynamic_slice_in_dim(gathered_design, start, records, axis=0)
    return (rotated_design, column_rms)


def solution(mesh):
    devices = mesh.devices.reshape(2, mesh.devices.shape[0] // 4, 2, 2, mesh.devices.shape[1] // 4, 2)
    view = Mesh(devices, COLUMN_AXES + RECORD_AXES)
    placed = (P(RECORD_AXES, COLUMN_AXES), P(RECORD_AXES))
    return jax.shard_map(
        local,
        mesh=view,
        in_specs=placed,
        out_specs=(P(RECORD_AXES, COLUMN_AXES), P(COLUMN_AXES)),
        check_vma=False,
    )
```

```python
import jax
import jax.numpy as jnp
from jax import lax
from jax.experimental import pallas as pl
from jax.experimental.pallas import tpu as pltpu
from jax.sharding import Mesh, PartitionSpec as P

ROUNDS = 3
SWEEPS = 6


eps_angle = 0.01


COLUMN_AXES = ("x_lo", "z", "core")
GROUP_AXES = ("x_hi", "y_hi")
PAIR_AXIS = "y_lo"
RECORD_AXES = GROUP_AXES + (PAIR_AXIS,)


def from_behind(value, steps):
    count = lax.axis_size(COLUMN_AXES)
    leading, last = (max(0, -steps), min(count, count - steps))
    return lax.ppermute(value, COLUMN_AXES, [(source, source + steps) for source in range(leading, last)])


PARTNER_AXES = ("core", "y_hi", PAIR_AXIS)


def partner_pairs(halves):
    pairs = []
    for half in range(halves):
        for core, other in ((0, half), (1, (half - 1) % halves)):
            even, odd = (core * halves + half) * 2, (core * halves + other) * 2 + 1
            pairs += [(even, odd), (odd, even)]
    return pairs


def from_partner(value):
    return lax.ppermute(value, PARTNER_AXES, partner_pairs(lax.axis_size("y_hi")))


def with_partner(value):
    return value + from_partner(value)


def diagonal_of(matrix):
    size = matrix.shape[0]
    rows = lax.broadcasted_iota(jnp.int32, (size, size), 0)
    cols = lax.broadcasted_iota(jnp.int32, (size, size), 1)
    return jnp.sum(jnp.where(rows == cols, matrix, 0.0), axis=0)


def half_angle_terms(first_diag, second_diag, coupling):
    spread = second_diag - first_diag
    tangent = (
        2.0
        * coupling
        * spread
        / (
            spread * spread
            + 4.0 * coupling * coupling
            + eps_angle * (first_diag + second_diag) ** 2
        )
    )
    double_cos = 1.0 / jnp.sqrt(1.0 + tangent * tangent)
    cosine = jnp.sqrt(0.5 + 0.5 * double_cos)
    sine_value = tangent * double_cos / (2.0 * cosine)
    return cosine, sine_value


def sweeps_kernel(local_ref, received_ref, rotation_ref):
    width = local_ref.shape[1]
    rows = lax.broadcasted_iota(jnp.int32, (width, width), 0)
    cols = lax.broadcasted_iota(jnp.int32, (width, width), 1)
    on_diagonal = rows == cols
    folded = local_ref[:width, :] + received_ref[:width, :]
    top_right = local_ref[width : 2 * width, :] + received_ref[width : 2 * width, :]
    low_diag = (local_ref[2 * width : 2 * width + 8, :] + received_ref[2 * width : 2 * width + 8, :])[:1, :]
    mirrored = folded.T
    top_left = jnp.where(rows <= cols, folded, mirrored)
    low_right = jnp.where(rows > cols, folded, jnp.where(rows < cols, mirrored, low_diag))
    low_left = top_right.T
    first_top = jnp.where(on_diagonal, 1.0, 0.0).astype(jnp.float32)
    first_low = jnp.zeros((width, width), jnp.float32)
    second_top = jnp.zeros((width, width), jnp.float32)
    second_low = first_top

    def diagonal_row(matrix):
        return jnp.sum(jnp.where(on_diagonal, matrix, 0.0), axis=0, keepdims=True)

    def as_column(row):
        return jnp.broadcast_to(row, (128, width)).T[:, :1]

    def to_left(matrix, axis):
        return pltpu.roll(matrix, width - 1, axis)

    for sweep_index in range(SWEEPS):
        if sweep_index > 0:
            top_right = to_left(top_right, 1)
            low_left = to_left(low_left, 0)
            low_right = to_left(to_left(low_right, 0), 1)
            second_top = to_left(second_top, 1)
            second_low = to_left(second_low, 1)
        cos_col, sin_col = half_angle_terms(
            diagonal_row(top_left), diagonal_row(low_right), diagonal_row(top_right)
        )
        cos_row = as_column(cos_col)
        sin_row = as_column(sin_col)
        left_a = top_left * cos_col - top_right * sin_col
        right_a = top_left * sin_col + top_right * cos_col
        left_b = low_left * cos_col - low_right * sin_col
        right_b = low_left * sin_col + low_right * cos_col
        top_left = cos_row * left_a - sin_row * left_b
        low_left = sin_row * left_a + cos_row * left_b
        top_right = cos_row * right_a - sin_row * right_b
        low_right = sin_row * right_a + cos_row * right_b
        first_top, second_top = (
            first_top * cos_col - second_top * sin_col,
            first_top * sin_col + second_top * cos_col,
        )
        first_low, second_low = (
            first_low * cos_col - second_low * sin_col,
            first_low * sin_col + second_low * cos_col,
        )
    second_top = pltpu.roll(second_top, SWEEPS - 1, 1)
    second_low = pltpu.roll(second_low, SWEEPS - 1, 1)
    out = rotation_ref.dtype
    rotation_ref[:width, :width] = first_top.astype(out)
    rotation_ref[width:, :width] = first_low.astype(out)
    rotation_ref[:width, width:] = second_top.astype(out)
    rotation_ref[width:, width:] = second_low.astype(out)


def rotation_of(local, received):
    width = local.shape[1]
    vmem = pl.BlockSpec(memory_space=pltpu.VMEM)
    return pl.pallas_call(
        sweeps_kernel,
        out_shape=jax.ShapeDtypeStruct((2 * width, 2 * width), jnp.bfloat16),
        in_specs=[vmem, vmem],
        out_specs=vmem,
        compiler_params=pltpu.CompilerParams(vmem_limit_bytes=16 * 1024 * 1024),
        cost_estimate=pl.CostEstimate(
            flops=SWEEPS * 40 * width * width, transcendentals=SWEEPS * 8 * width, bytes_accessed=4 * 4 * width * width
        ),
    )(local, received)


def send_right(block):
    return from_behind(block, 1)


def send_left(block):
    return from_behind(block, -1)


def inner_products(left_part, right_part):
    return lax.dot_general(
        left_part, right_part, (((0,), (0,)), ((), ())), preferred_element_type=jnp.float32
    )


def gathered_records(block):
    count = lax.axis_size(GROUP_AXES)
    spread = jnp.broadcast_to(block[None], (count,) + block.shape)
    gathered = lax.all_to_all(spread, GROUP_AXES, 0, 0, tiled=False)
    return gathered.reshape(count * block.shape[0], block.shape[1])


def summed_gram(pair_data, width):
    gram_local = inner_products(pair_data, pair_data)
    top_left = gram_local[:width, :width]
    top_right = gram_local[:width, width:]
    low_right = gram_local[width:, width:]
    rows = lax.broadcasted_iota(jnp.int32, (width, width), 0)
    cols = lax.broadcasted_iota(jnp.int32, (width, width), 1)
    folded = jnp.where(rows <= cols, top_left, low_right)
    padded = -(-(2 * width + 1) // 8) * 8
    packed = jnp.concatenate(
        [
            folded,
            top_right,
            diagonal_of(low_right)[None, :],
            jnp.zeros((padded - 2 * width - 1, width), jnp.float32),
        ],
        axis=0,
    )
    return packed, from_partner(packed)


def local(design, record_weight):
    width = design.shape[1] // 2
    records = design.shape[0]
    weighted = (design.astype(jnp.float32) * record_weight[:, None]).astype(jnp.bfloat16)
    weighted = gathered_records(weighted)
    upper_block = weighted[:, :width]
    lower_block = weighted[:, width:]
    position = lax.axis_index(COLUMN_AXES)
    device_count = lax.axis_size(COLUMN_AXES)
    for round_index in range(ROUNDS):
        moving = round_index + 1 < ROUNDS
        pair_data = jnp.concatenate([upper_block, lower_block], axis=1)
        rotation = rotation_of(*summed_gram(pair_data, width))
        if not moving:
            rotated = jnp.dot(pair_data, rotation, preferred_element_type=jnp.float32)
            upper_block = rotated[:, :width].astype(jnp.bfloat16)
            lower_block = rotated[:, width:].astype(jnp.bfloat16)
            break
        first_columns = rotation[:, :width]
        second_columns = rotation[:, width:]
        going_right = jnp.dot(
            pair_data,
            jnp.where(position == 0, second_columns, first_columns),
            preferred_element_type=jnp.float32,
        ).astype(jnp.bfloat16)
        going_left = jnp.dot(
            pair_data,
            jnp.where(position == 0, first_columns, second_columns),
            preferred_element_type=jnp.float32,
        ).astype(jnp.bfloat16)
        from_left = send_right(going_right)
        from_right = send_left(going_left)
        upper_block = jnp.where(position == 0, going_left, from_left)
        lower_block = jnp.where(position == device_count - 1, going_right, from_right)
    gathered_design = jnp.concatenate([upper_block, lower_block], axis=1)
    squares = with_partner(jnp.sum(jnp.square(gathered_design.astype(jnp.float32)), axis=0))
    record_total = records * lax.axis_size(RECORD_AXES)
    column_rms = jnp.sqrt(squares / record_total + 1e-06)
    start = lax.axis_index(GROUP_AXES) * records
    rotated_design = lax.dynamic_slice_in_dim(gathered_design, start, records, axis=0)
    return (rotated_design, column_rms)


def solution(mesh):
    devices = mesh.devices.reshape(2, mesh.devices.shape[0] // 4, 2, 2, mesh.devices.shape[1] // 4, 2)
    view = Mesh(devices, COLUMN_AXES + RECORD_AXES)
    placed = (P(RECORD_AXES, COLUMN_AXES), P(RECORD_AXES))
    return jax.shard_map(
        local,
        mesh=view,
        in_specs=placed,
        out_specs=(P(RECORD_AXES, COLUMN_AXES), P(COLUMN_AXES)),
        check_vma=False,
    )
```

```python
import jax
import jax.numpy as jnp
from jax import lax
from jax.experimental import pallas as pl
from jax.experimental.pallas import tpu as pltpu
from jax.sharding import Mesh, PartitionSpec as P

ROUNDS = 3
SWEEPS = 6


eps_angle = 0.01


COLUMN_AXES = ("x_lo", "z", "core")
GROUP_AXES = ("x_hi", "y_hi")
PAIR_AXIS = "y_lo"
RECORD_AXES = GROUP_AXES + (PAIR_AXIS,)


def from_behind(value, steps):
    count = lax.axis_size(COLUMN_AXES)
    leading, last = (max(0, -steps), min(count, count - steps))
    return lax.ppermute(value, COLUMN_AXES, [(source, source + steps) for source in range(leading, last)])


PARTNER_AXES = ("core", "y_hi", PAIR_AXIS)


def partner_pairs(halves):
    pairs = []
    for half in range(halves):
        for core, other in ((0, half), (1, (half - 1) % halves)):
            even, odd = (core * halves + half) * 2, (core * halves + other) * 2 + 1
            pairs += [(even, odd), (odd, even)]
    return pairs


def from_partner(value):
    return lax.ppermute(value, PARTNER_AXES, partner_pairs(lax.axis_size("y_hi")))


def with_partner(value):
    return value + from_partner(value)


def diagonal_of(matrix):
    size = matrix.shape[0]
    rows = lax.broadcasted_iota(jnp.int32, (size, size), 0)
    cols = lax.broadcasted_iota(jnp.int32, (size, size), 1)
    return jnp.sum(jnp.where(rows == cols, matrix, 0.0), axis=0)


def half_angle_terms(first_diag, second_diag, coupling):
    spread = second_diag - first_diag
    tangent = (
        2.0
        * coupling
        * spread
        / (
            spread * spread
            + 4.0 * coupling * coupling
            + eps_angle * (first_diag + second_diag) ** 2
        )
    )
    double_cos = 1.0 / jnp.sqrt(1.0 + tangent * tangent)
    cosine = jnp.sqrt(0.5 + 0.5 * double_cos)
    sine_value = tangent * double_cos / (2.0 * cosine)
    return cosine, sine_value


def sweeps_kernel(local_ref, received_ref, rotation_ref):
    width = local_ref.shape[1]
    rows = lax.broadcasted_iota(jnp.int32, (width, width), 0)
    cols = lax.broadcasted_iota(jnp.int32, (width, width), 1)
    on_diagonal = rows == cols
    folded = local_ref[:width, :] + received_ref[:width, :]
    top_right = local_ref[width : 2 * width, :] + received_ref[width : 2 * width, :]
    low_diag = (local_ref[2 * width : 2 * width + 8, :] + received_ref[2 * width : 2 * width + 8, :])[:1, :]
    mirrored = folded.T
    top_left = jnp.where(rows <= cols, folded, mirrored)
    low_right = jnp.where(rows > cols, folded, jnp.where(rows < cols, mirrored, low_diag))
    first_top = jnp.where(on_diagonal, 1.0, 0.0).astype(jnp.float32)
    first_low = jnp.zeros((width, width), jnp.float32)
    second_top = jnp.zeros((width, width), jnp.float32)
    second_low = first_top

    def diagonal_row(matrix):
        return jnp.sum(jnp.where(on_diagonal, matrix, 0.0), axis=0, keepdims=True)

    def as_column(row):
        return jnp.broadcast_to(row, (128, width)).T[:, :1]

    def to_left(matrix, axis):
        return pltpu.roll(matrix, width - 1, axis)

    for sweep_index in range(SWEEPS):
        if sweep_index > 0:
            top_right = to_left(top_right, 1)
            low_right = to_left(to_left(low_right, 0), 1)
            second_top = to_left(second_top, 1)
            second_low = to_left(second_low, 1)
        low_left = top_right.T
        cos_col, sin_col = half_angle_terms(
            diagonal_row(top_left), diagonal_row(low_right), diagonal_row(top_right)
        )
        cos_row = as_column(cos_col)
        sin_row = as_column(sin_col)
        left_a = top_left * cos_col - top_right * sin_col
        right_a = top_left * sin_col + top_right * cos_col
        left_b = low_left * cos_col - low_right * sin_col
        right_b = low_left * sin_col + low_right * cos_col
        top_left = cos_row * left_a - sin_row * left_b
        top_right = cos_row * right_a - sin_row * right_b
        low_right = sin_row * right_a + cos_row * right_b
        first_top, second_top = (
            first_top * cos_col - second_top * sin_col,
            first_top * sin_col + second_top * cos_col,
        )
        first_low, second_low = (
            first_low * cos_col - second_low * sin_col,
            first_low * sin_col + second_low * cos_col,
        )
    second_top = pltpu.roll(second_top, SWEEPS - 1, 1)
    second_low = pltpu.roll(second_low, SWEEPS - 1, 1)
    out = rotation_ref.dtype
    rotation_ref[:width, :width] = first_top.astype(out)
    rotation_ref[width:, :width] = first_low.astype(out)
    rotation_ref[:width, width:] = second_top.astype(out)
    rotation_ref[width:, width:] = second_low.astype(out)


def rotation_of(local, received):
    width = local.shape[1]
    vmem = pl.BlockSpec(memory_space=pltpu.VMEM)
    return pl.pallas_call(
        sweeps_kernel,
        out_shape=jax.ShapeDtypeStruct((2 * width, 2 * width), jnp.bfloat16),
        in_specs=[vmem, vmem],
        out_specs=vmem,
        compiler_params=pltpu.CompilerParams(vmem_limit_bytes=16 * 1024 * 1024),
        cost_estimate=pl.CostEstimate(
            flops=SWEEPS * 40 * width * width, transcendentals=SWEEPS * 8 * width, bytes_accessed=4 * 4 * width * width
        ),
    )(local, received)


def send_right(block):
    return from_behind(block, 1)


def send_left(block):
    return from_behind(block, -1)


def inner_products(left_part, right_part):
    return lax.dot_general(
        left_part, right_part, (((0,), (0,)), ((), ())), preferred_element_type=jnp.float32
    )


def gathered_records(block):
    count = lax.axis_size(GROUP_AXES)
    spread = jnp.broadcast_to(block[None], (count,) + block.shape)
    gathered = lax.all_to_all(spread, GROUP_AXES, 0, 0, tiled=False)
    return gathered.reshape(count * block.shape[0], block.shape[1])


def summed_gram(pair_data, width):
    gram_local = inner_products(pair_data, pair_data)
    top_left = gram_local[:width, :width]
    top_right = gram_local[:width, width:]
    low_right = gram_local[width:, width:]
    rows = lax.broadcasted_iota(jnp.int32, (width, width), 0)
    cols = lax.broadcasted_iota(jnp.int32, (width, width), 1)
    folded = jnp.where(rows <= cols, top_left, low_right)
    padded = -(-(2 * width + 1) // 8) * 8
    packed = jnp.concatenate(
        [
            folded,
            top_right,
            diagonal_of(low_right)[None, :],
            jnp.zeros((padded - 2 * width - 1, width), jnp.float32),
        ],
        axis=0,
    )
    return packed, from_partner(packed)


def local(design, record_weight):
    width = design.shape[1] // 2
    records = design.shape[0]
    weighted = (design.astype(jnp.float32) * record_weight[:, None]).astype(jnp.bfloat16)
    weighted = gathered_records(weighted)
    upper_block = weighted[:, :width]
    lower_block = weighted[:, width:]
    position = lax.axis_index(COLUMN_AXES)
    device_count = lax.axis_size(COLUMN_AXES)
    for round_index in range(ROUNDS):
        moving = round_index + 1 < ROUNDS
        pair_data = jnp.concatenate([upper_block, lower_block], axis=1)
        rotation = rotation_of(*summed_gram(pair_data, width))
        if not moving:
            rotated = jnp.dot(pair_data, rotation, preferred_element_type=jnp.float32)
            upper_block = rotated[:, :width].astype(jnp.bfloat16)
            lower_block = rotated[:, width:].astype(jnp.bfloat16)
            break
        first_columns = rotation[:, :width]
        second_columns = rotation[:, width:]
        going_right = jnp.dot(
            pair_data,
            jnp.where(position == 0, second_columns, first_columns),
            preferred_element_type=jnp.float32,
        ).astype(jnp.bfloat16)
        going_left = jnp.dot(
            pair_data,
            jnp.where(position == 0, first_columns, second_columns),
            preferred_element_type=jnp.float32,
        ).astype(jnp.bfloat16)
        from_left = send_right(going_right)
        from_right = send_left(going_left)
        upper_block = jnp.where(position == 0, going_left, from_left)
        lower_block = jnp.where(position == device_count - 1, going_right, from_right)
    gathered_design = jnp.concatenate([upper_block, lower_block], axis=1)
    squares = with_partner(jnp.sum(jnp.square(gathered_design.astype(jnp.float32)), axis=0))
    record_total = records * lax.axis_size(RECORD_AXES)
    column_rms = jnp.sqrt(squares / record_total + 1e-06)
    start = lax.axis_index(GROUP_AXES) * records
    rotated_design = lax.dynamic_slice_in_dim(gathered_design, start, records, axis=0)
    return (rotated_design, column_rms)


def solution(mesh):
    devices = mesh.devices.reshape(2, mesh.devices.shape[0] // 4, 2, 2, mesh.devices.shape[1] // 4, 2)
    view = Mesh(devices, COLUMN_AXES + RECORD_AXES)
    placed = (P(RECORD_AXES, COLUMN_AXES), P(RECORD_AXES))
    return jax.shard_map(
        local,
        mesh=view,
        in_specs=placed,
        out_specs=(P(RECORD_AXES, COLUMN_AXES), P(COLUMN_AXES)),
        check_vma=False,
    )
```

```python
import jax
import jax.numpy as jnp
from jax import lax
from jax.experimental import pallas as pl
from jax.experimental.pallas import tpu as pltpu
from jax.sharding import Mesh, PartitionSpec as P

ROUNDS = 3
SWEEPS = 6


eps_angle = 0.01


COLUMN_AXES = ("x_lo", "z", "core")
GROUP_AXES = ("x_hi", "y_hi")
PAIR_AXIS = "y_lo"
RECORD_AXES = GROUP_AXES + (PAIR_AXIS,)


def from_behind(value, steps):
    count = lax.axis_size(COLUMN_AXES)
    leading, last = (max(0, -steps), min(count, count - steps))
    return lax.ppermute(value, COLUMN_AXES, [(source, source + steps) for source in range(leading, last)])


PARTNER_AXES = ("core", "y_hi", PAIR_AXIS)


def partner_pairs(halves):
    pairs = []
    for half in range(halves):
        for core, other in ((0, half), (1, (half - 1) % halves)):
            even, odd = (core * halves + half) * 2, (core * halves + other) * 2 + 1
            pairs += [(even, odd), (odd, even)]
    return pairs


def from_partner(value):
    return lax.ppermute(value, PARTNER_AXES, partner_pairs(lax.axis_size("y_hi")))


def with_partner(value):
    return value + from_partner(value)


def diagonal_of(matrix):
    size = matrix.shape[0]
    rows = lax.broadcasted_iota(jnp.int32, (size, size), 0)
    cols = lax.broadcasted_iota(jnp.int32, (size, size), 1)
    return jnp.sum(jnp.where(rows == cols, matrix, 0.0), axis=0)


def half_angle_terms(first_diag, second_diag, coupling):
    spread = second_diag - first_diag
    tangent = (
        2.0
        * coupling
        * spread
        / (
            spread * spread
            + 4.0 * coupling * coupling
            + eps_angle * (first_diag + second_diag) ** 2
        )
    )
    double_cos = 1.0 / jnp.sqrt(1.0 + tangent * tangent)
    cosine = jnp.sqrt(0.5 + 0.5 * double_cos)
    sine_value = tangent * double_cos / (2.0 * cosine)
    return cosine, sine_value


def sweeps_kernel(local_ref, received_ref, rotation_ref):
    width = local_ref.shape[1]
    rows = lax.broadcasted_iota(jnp.int32, (width, width), 0)
    cols = lax.broadcasted_iota(jnp.int32, (width, width), 1)
    on_diagonal = rows == cols
    folded = local_ref[:width, :] + received_ref[:width, :]
    top_right = local_ref[width : 2 * width, :] + received_ref[width : 2 * width, :]
    low_diag = (local_ref[2 * width : 2 * width + 8, :] + received_ref[2 * width : 2 * width + 8, :])[:1, :]
    mirrored = folded.T
    top_left = jnp.where(rows <= cols, folded, mirrored)
    low_right = jnp.where(rows > cols, folded, jnp.where(rows < cols, mirrored, low_diag))
    first_top = jnp.where(on_diagonal, 1.0, 0.0).astype(jnp.float32)
    first_low = jnp.zeros((width, width), jnp.float32)
    second_top = jnp.zeros((width, width), jnp.float32)
    second_low = first_top

    def diagonal_row(matrix):
        return jnp.sum(jnp.where(on_diagonal, matrix, 0.0), axis=0, keepdims=True)

    def as_column(row):
        return jnp.broadcast_to(row, (128, width)).T[:, :1]

    def to_left(matrix, axis):
        return pltpu.roll(matrix, width - 1, axis)

    for sweep_index in range(SWEEPS):
        if sweep_index > 0:
            top_right = to_left(top_right, 1)
            low_right = to_left(to_left(low_right, 0), 1)
            second_top = to_left(second_top, 1)
            second_low = to_left(second_low, 1)
        low_left = top_right.T
        cos_col, sin_col = half_angle_terms(
            diagonal_row(top_left), diagonal_row(low_right), diagonal_row(top_right)
        )
        cos_row = as_column(cos_col)
        sin_row = as_column(sin_col)
        left_a = top_left * cos_col - top_right * sin_col
        right_a = top_left * sin_col + top_right * cos_col
        left_b = low_left * cos_col - low_right * sin_col
        right_b = low_left * sin_col + low_right * cos_col
        top_left = cos_row * left_a - sin_row * left_b
        top_right = cos_row * right_a - sin_row * right_b
        low_right = sin_row * right_a + cos_row * right_b
        if sweep_index == 0:
            first_top, second_top = first_top * cos_col, first_top * sin_col
            first_low, second_low = -(second_low * sin_col), second_low * cos_col
        else:
            first_top, second_top = (
                first_top * cos_col - second_top * sin_col,
                first_top * sin_col + second_top * cos_col,
            )
            first_low, second_low = (
                first_low * cos_col - second_low * sin_col,
                first_low * sin_col + second_low * cos_col,
            )
    second_top = pltpu.roll(second_top, SWEEPS - 1, 1)
    second_low = pltpu.roll(second_low, SWEEPS - 1, 1)
    out = rotation_ref.dtype
    rotation_ref[:width, :width] = first_top.astype(out)
    rotation_ref[width:, :width] = first_low.astype(out)
    rotation_ref[:width, width:] = second_top.astype(out)
    rotation_ref[width:, width:] = second_low.astype(out)


def rotation_of(local, received):
    width = local.shape[1]
    vmem = pl.BlockSpec(memory_space=pltpu.VMEM)
    return pl.pallas_call(
        sweeps_kernel,
        out_shape=jax.ShapeDtypeStruct((2 * width, 2 * width), jnp.bfloat16),
        in_specs=[vmem, vmem],
        out_specs=vmem,
        compiler_params=pltpu.CompilerParams(vmem_limit_bytes=16 * 1024 * 1024),
        cost_estimate=pl.CostEstimate(
            flops=SWEEPS * 40 * width * width, transcendentals=SWEEPS * 8 * width, bytes_accessed=4 * 4 * width * width
        ),
    )(local, received)


def send_right(block):
    return from_behind(block, 1)


def send_left(block):
    return from_behind(block, -1)


def inner_products(left_part, right_part):
    return lax.dot_general(
        left_part, right_part, (((0,), (0,)), ((), ())), preferred_element_type=jnp.float32
    )


def gathered_records(block):
    count = lax.axis_size(GROUP_AXES)
    spread = jnp.broadcast_to(block[None], (count,) + block.shape)
    gathered = lax.all_to_all(spread, GROUP_AXES, 0, 0, tiled=False)
    return gathered.reshape(count * block.shape[0], block.shape[1])


def summed_gram(pair_data, width):
    gram_local = inner_products(pair_data, pair_data)
    top_left = gram_local[:width, :width]
    top_right = gram_local[:width, width:]
    low_right = gram_local[width:, width:]
    rows = lax.broadcasted_iota(jnp.int32, (width, width), 0)
    cols = lax.broadcasted_iota(jnp.int32, (width, width), 1)
    folded = jnp.where(rows <= cols, top_left, low_right)
    padded = -(-(2 * width + 1) // 8) * 8
    packed = jnp.concatenate(
        [
            folded,
            top_right,
            diagonal_of(low_right)[None, :],
            jnp.zeros((padded - 2 * width - 1, width), jnp.float32),
        ],
        axis=0,
    )
    return packed, from_partner(packed)


def local(design, record_weight):
    width = design.shape[1] // 2
    records = design.shape[0]
    weighted = (design.astype(jnp.float32) * record_weight[:, None]).astype(jnp.bfloat16)
    weighted = gathered_records(weighted)
    upper_block = weighted[:, :width]
    lower_block = weighted[:, width:]
    position = lax.axis_index(COLUMN_AXES)
    device_count = lax.axis_size(COLUMN_AXES)
    for round_index in range(ROUNDS):
        moving = round_index + 1 < ROUNDS
        pair_data = jnp.concatenate([upper_block, lower_block], axis=1)
        rotation = rotation_of(*summed_gram(pair_data, width))
        if not moving:
            rotated = jnp.dot(pair_data, rotation, preferred_element_type=jnp.float32)
            upper_block = rotated[:, :width].astype(jnp.bfloat16)
            lower_block = rotated[:, width:].astype(jnp.bfloat16)
            break
        first_columns = rotation[:, :width]
        second_columns = rotation[:, width:]
        going_right = jnp.dot(
            pair_data,
            jnp.where(position == 0, second_columns, first_columns),
            preferred_element_type=jnp.float32,
        ).astype(jnp.bfloat16)
        going_left = jnp.dot(
            pair_data,
            jnp.where(position == 0, first_columns, second_columns),
            preferred_element_type=jnp.float32,
        ).astype(jnp.bfloat16)
        from_left = send_right(going_right)
        from_right = send_left(going_left)
        upper_block = jnp.where(position == 0, going_left, from_left)
        lower_block = jnp.where(position == device_count - 1, going_right, from_right)
    gathered_design = jnp.concatenate([upper_block, lower_block], axis=1)
    squares = with_partner(jnp.sum(jnp.square(gathered_design.astype(jnp.float32)), axis=0))
    record_total = records * lax.axis_size(RECORD_AXES)
    column_rms = jnp.sqrt(squares / record_total + 1e-06)
    start = lax.axis_index(GROUP_AXES) * records
    rotated_design = lax.dynamic_slice_in_dim(gathered_design, start, records, axis=0)
    return (rotated_design, column_rms)


def solution(mesh):
    devices = mesh.devices.reshape(2, mesh.devices.shape[0] // 4, 2, 2, mesh.devices.shape[1] // 4, 2)
    view = Mesh(devices, COLUMN_AXES + RECORD_AXES)
    placed = (P(RECORD_AXES, COLUMN_AXES), P(RECORD_AXES))
    return jax.shard_map(
        local,
        mesh=view,
        in_specs=placed,
        out_specs=(P(RECORD_AXES, COLUMN_AXES), P(COLUMN_AXES)),
        check_vma=False,
    )
```

```python
import jax
import jax.numpy as jnp
from jax import lax
from jax.experimental import pallas as pl
from jax.experimental.pallas import tpu as pltpu
from jax.sharding import Mesh, PartitionSpec as P

ROUNDS = 3
SWEEPS = 6


eps_angle = 0.01


COLUMN_AXES = ("x_lo", "z", "core")
GROUP_AXES = ("x_hi", "y_hi")
PAIR_AXIS = "y_lo"
RECORD_AXES = GROUP_AXES + (PAIR_AXIS,)


def from_behind(value, steps):
    count = lax.axis_size(COLUMN_AXES)
    leading, last = (max(0, -steps), min(count, count - steps))
    return lax.ppermute(value, COLUMN_AXES, [(source, source + steps) for source in range(leading, last)])


PARTNER_AXES = ("core", "y_hi", PAIR_AXIS)


def partner_pairs(halves):
    pairs = []
    for half in range(halves):
        for core, other in ((0, half), (1, (half - 1) % halves)):
            even, odd = (core * halves + half) * 2, (core * halves + other) * 2 + 1
            pairs += [(even, odd), (odd, even)]
    return pairs


def from_partner(value):
    return lax.ppermute(value, PARTNER_AXES, partner_pairs(lax.axis_size("y_hi")))


def with_partner(value):
    return value + from_partner(value)


def diagonal_of(matrix):
    size = matrix.shape[0]
    rows = lax.broadcasted_iota(jnp.int32, (size, size), 0)
    cols = lax.broadcasted_iota(jnp.int32, (size, size), 1)
    return jnp.sum(jnp.where(rows == cols, matrix, 0.0), axis=0)


def half_angle_terms(first_diag, second_diag, coupling):
    spread = second_diag - first_diag
    tangent = (
        2.0
        * coupling
        * spread
        / (
            spread * spread
            + 4.0 * coupling * coupling
            + eps_angle * (first_diag + second_diag) ** 2
        )
    )
    double_cos = 1.0 / jnp.sqrt(1.0 + tangent * tangent)
    cosine = jnp.sqrt(0.5 + 0.5 * double_cos)
    sine_value = tangent * double_cos / (2.0 * cosine)
    return cosine, sine_value


def sweeps_kernel(local_ref, received_ref, rotation_ref):
    width = local_ref.shape[1]
    rows = lax.broadcasted_iota(jnp.int32, (width, width), 0)
    cols = lax.broadcasted_iota(jnp.int32, (width, width), 1)
    on_diagonal = rows == cols
    folded = local_ref[:width, :] + received_ref[:width, :]
    top_right = local_ref[width : 2 * width, :] + received_ref[width : 2 * width, :]
    low_diag = (local_ref[2 * width : 2 * width + 8, :] + received_ref[2 * width : 2 * width + 8, :])[:1, :]
    mirrored = folded.T
    top_left = jnp.where(rows <= cols, folded, mirrored)
    low_right = jnp.where(rows > cols, folded, jnp.where(rows < cols, mirrored, low_diag))
    first_top = jnp.where(on_diagonal, 1.0, 0.0).astype(jnp.float32)
    first_low = jnp.zeros((width, width), jnp.float32)
    second_top = jnp.zeros((width, width), jnp.float32)
    second_low = first_top

    def diagonal_row(matrix):
        return jnp.sum(jnp.where(on_diagonal, matrix, 0.0), axis=0, keepdims=True)

    def as_column(row):
        return jnp.broadcast_to(row, (128, width)).T[:, :1]

    def to_left(matrix, axis):
        return pltpu.roll(matrix, width - 1, axis)

    for sweep_index in range(SWEEPS):
        if sweep_index > 0:
            top_right = to_left(top_right, 1)
            low_right = to_left(to_left(low_right, 0), 1)
            second_top = to_left(second_top, 1)
            second_low = to_left(second_low, 1)
        low_left = top_right.T
        cos_col, sin_col = half_angle_terms(
            diagonal_row(top_left), diagonal_row(low_right), diagonal_row(top_right)
        )
        cos_row = as_column(cos_col)
        sin_row = as_column(sin_col)
        left_a = top_left * cos_col - top_right * sin_col
        right_a = top_left * sin_col + top_right * cos_col
        left_b = low_left * cos_col - low_right * sin_col
        right_b = low_left * sin_col + low_right * cos_col
        top_left = cos_row * left_a - sin_row * left_b
        top_right = cos_row * right_a - sin_row * right_b
        low_right = sin_row * right_a + cos_row * right_b
        first_top, second_top = (
            first_top * cos_col - second_top * sin_col,
            first_top * sin_col + second_top * cos_col,
        )
        first_low, second_low = (
            first_low * cos_col - second_low * sin_col,
            first_low * sin_col + second_low * cos_col,
        )
    second_top = pltpu.roll(second_top, SWEEPS - 1, 1)
    second_low = pltpu.roll(second_low, SWEEPS - 1, 1)
    out = rotation_ref.dtype
    rotation_ref[:width, :width] = first_top.astype(out)
    rotation_ref[width:, :width] = first_low.astype(out)
    rotation_ref[:width, width:] = second_top.astype(out)
    rotation_ref[width:, width:] = second_low.astype(out)


def rotation_of(local, received):
    width = local.shape[1]
    vmem = pl.BlockSpec(memory_space=pltpu.VMEM)
    return pl.pallas_call(
        sweeps_kernel,
        out_shape=jax.ShapeDtypeStruct((2 * width, 2 * width), jnp.bfloat16),
        in_specs=[vmem, vmem],
        out_specs=vmem,
        compiler_params=pltpu.CompilerParams(vmem_limit_bytes=16 * 1024 * 1024),
        cost_estimate=pl.CostEstimate(
            flops=SWEEPS * 40 * width * width, transcendentals=SWEEPS * 8 * width, bytes_accessed=4 * 4 * width * width
        ),
    )(local, received)


def send_right(block):
    return from_behind(block, 1)


def send_left(block):
    return from_behind(block, -1)


def inner_products(left_part, right_part):
    return lax.dot_general(
        left_part, right_part, (((0,), (0,)), ((), ())), preferred_element_type=jnp.float32
    )


def gathered_records(block):
    count = lax.axis_size(GROUP_AXES)
    spread = jnp.broadcast_to(block[None], (count,) + block.shape)
    gathered = lax.all_to_all(spread, GROUP_AXES, 0, 0, tiled=False)
    return gathered.reshape(count * block.shape[0], block.shape[1])


def summed_gram(pair_data, width):
    gram_local = inner_products(pair_data, pair_data)
    top_left = gram_local[:width, :width]
    top_right = gram_local[:width, width:]
    low_right = gram_local[width:, width:]
    rows = lax.broadcasted_iota(jnp.int32, (width, width), 0)
    cols = lax.broadcasted_iota(jnp.int32, (width, width), 1)
    folded = jnp.where(rows <= cols, top_left, low_right)
    padded = -(-(2 * width + 1) // 8) * 8
    packed = jnp.concatenate(
        [
            folded,
            top_right,
            diagonal_of(low_right)[None, :],
            jnp.zeros((padded - 2 * width - 1, width), jnp.float32),
        ],
        axis=0,
    )
    return packed, from_partner(packed)


def local(design, record_weight):
    width = design.shape[1] // 2
    records = design.shape[0]
    weighted = (design.astype(jnp.float32) * record_weight[:, None]).astype(jnp.bfloat16)
    weighted = gathered_records(weighted)
    upper_block = weighted[:, :width]
    lower_block = weighted[:, width:]
    position = lax.axis_index(COLUMN_AXES)
    device_count = lax.axis_size(COLUMN_AXES)
    for round_index in range(ROUNDS):
        moving = round_index + 1 < ROUNDS
        pair_data = jnp.concatenate([upper_block, lower_block], axis=1)
        rotation = rotation_of(*summed_gram(pair_data, width))
        if not moving:
            break
        first_columns = rotation[:, :width]
        second_columns = rotation[:, width:]
        going_right = jnp.dot(
            pair_data,
            jnp.where(position == 0, second_columns, first_columns),
            preferred_element_type=jnp.float32,
        ).astype(jnp.bfloat16)
        going_left = jnp.dot(
            pair_data,
            jnp.where(position == 0, first_columns, second_columns),
            preferred_element_type=jnp.float32,
        ).astype(jnp.bfloat16)
        from_left = send_right(going_right)
        from_right = send_left(going_left)
        upper_block = jnp.where(position == 0, going_left, from_left)
        lower_block = jnp.where(position == device_count - 1, going_right, from_right)
    rotated = jnp.dot(pair_data, rotation, preferred_element_type=jnp.float32).astype(jnp.bfloat16)
    squares = with_partner(jnp.sum(jnp.square(rotated.astype(jnp.float32)), axis=0))
    record_total = records * lax.axis_size(RECORD_AXES)
    column_rms = jnp.sqrt(squares / record_total + 1e-06)
    start = lax.axis_index(GROUP_AXES) * records
    own_rows = lax.dynamic_slice_in_dim(pair_data, start, records, axis=0)
    rotated_design = jnp.dot(own_rows, rotation, preferred_element_type=jnp.float32).astype(jnp.bfloat16)
    return (rotated_design, column_rms)


def solution(mesh):
    devices = mesh.devices.reshape(2, mesh.devices.shape[0] // 4, 2, 2, mesh.devices.shape[1] // 4, 2)
    view = Mesh(devices, COLUMN_AXES + RECORD_AXES)
    placed = (P(RECORD_AXES, COLUMN_AXES), P(RECORD_AXES))
    return jax.shard_map(
        local,
        mesh=view,
        in_specs=placed,
        out_specs=(P(RECORD_AXES, COLUMN_AXES), P(COLUMN_AXES)),
        check_vma=False,
    )
```
